256 devices in a mesh: prow: 8 (over x, core), pcol: 32 (over y, z).
Axes of the slice: x: 4, y: 4, z: 8, core: 2. Of those that a mesh axis runs over, the one named last changes fastest.
Arguments:
- factor: bfloat16 [16, 8, 4, 32, 256, 256], P(None, 'prow', None, 'pcol')
- right_side: bfloat16 [4, 32, 256, 256], P(None, 'pcol'), may hold values from -6 to 6
- node_blocks: int32 [15], replicated, may hold values from 1 to 32, as said below
- front_mask: int32 [15, 128], replicated, may hold values from 0 to 1, as said below
Outputs:
- solution: bfloat16 [4, 32, 256, 256], P(None, 'pcol')
The draws below stay inside these ranges and needn't reach their ends.
Inputs may be any that keep to these rules, and one draw needn't show every extreme that they name: node_blocks[s] counts the blocks of node s of a complete binary elimination tree in heap order (the parent of s is (s - 1) // 2); the nodes of one depth together have 32 blocks. front_mask[s, i] is 1 only where block i belongs to a strict ancestor of node s.
All inputs are finite; a program needn't handle non-finite values.
Results may differ from the reference program's by a relative error of at most 0.024.
Values may be sent and summed in bfloat16 or wider, within the bound.
No kernel may reach another device: no remote copies, remote signals or barrier semaphores. Data moves between devices by JAX's collectives and lax.ppermute only.
A program may use at most 128 MiB of HBM per device.

```python
import math
import jax
import jax.numpy as jnp
import numpy as np
from jax import lax

LEVELS = 4
BS = 256
NRHS = 256
K = 32
NB = 128
NODES = 15
N_PROW = 8
N_PCOL = 32


def node_order_drawn():
    ordering = []
    for depth_now in range(LEVELS - 1, -1, -1):
        ordering.extend(range(2 ** depth_now - 1, 2 ** (depth_now + 1) - 1))
    return ordering


def node_table_drawn(node_blocks, total_blocks):
    node_count = node_blocks.shape[0]
    ordered = jnp.array(node_order_drawn(), dtype=jnp.int32)
    node_ids = jnp.arange(node_count, dtype=jnp.int32)
    pick_sizes = (ordered[:, None] == node_ids[None, :]).astype(jnp.int32)
    level_sizes = jnp.sum(pick_sizes * node_blocks[None, :], axis=1).astype(jnp.int32)
    block_ends = jnp.cumsum(level_sizes).astype(jnp.int32)
    block_ids = jnp.arange(total_blocks, dtype=jnp.int32)
    positions = jnp.sum((block_ids[:, None] >= block_ends[None, :]).astype(jnp.int32), axis=1).astype(jnp.int32)
    return jnp.sum((positions[:, None] == node_ids[None, :]).astype(jnp.int32) * ordered[None, :], axis=1).astype(jnp.int32)


def tree_sizes(key):
    sizes_key = jax.random.fold_in(key, 11)
    pieces_list = [jnp.full((1,), K, jnp.int32)]
    for depth_now in range(1, LEVELS):
        node_count = 2 ** depth_now
        level_key = jax.random.fold_in(sizes_key, depth_now)
        cut_points = jnp.sort(jax.random.permutation(level_key, K - 1)[:node_count - 1] + 1).astype(jnp.int32)
        boundaries = jnp.concatenate([jnp.zeros((1,), jnp.int32), cut_points, jnp.full((1,), K, jnp.int32)])
        pieces_list.append(boundaries[1:] - boundaries[:-1])
    return jnp.concatenate(pieces_list).astype(jnp.int32)


def ancestor_table():
    table_rows = []
    for node_now in range(NODES):
        ancestor_marks = [0] * NODES
        walker = node_now
        while walker > 0:
            walker = (walker - 1) // 2
            ancestor_marks[walker] = 1
        table_rows.append(ancestor_marks)
    return np.array(table_rows, dtype=np.int32)


def draw_node_blocks(key, part):
    return tree_sizes(key)


def draw_front_mask(key, part):
    block_node = node_table_drawn(tree_sizes(key), NB)
    ancestors = jnp.asarray(ancestor_table())
    node_ids = jnp.arange(NODES, dtype=jnp.int32)
    onehot_nodes = (block_node[:, None] == node_ids[None, :]).astype(jnp.int32)
    ancestor_blocks = jnp.sum(ancestors[:, None, :] * onehot_nodes[None, :, :], axis=2)
    coins = jax.random.randint(jax.random.fold_in(key, 23), (NODES, NB), 0, 4)
    return (ancestor_blocks * (coins < 3).astype(jnp.int32)).astype(jnp.int32)


def draw_factor(key, part):
    spread = 0.7 / math.sqrt(K * BS)
    full_shape = (NB, NB, BS, BS)
    entries = jax.random.normal(key, full_shape, jnp.float32) * spread
    same_block = (jnp.arange(NB)[:, None] == jnp.arange(NB)[None, :]).astype(jnp.float32)
    entries = entries + same_block[:, :, None, None] * jnp.eye(BS, dtype=jnp.float32)[None, None, :, :]
    return entries.reshape(NB // N_PROW, N_PROW, NB // N_PCOL, N_PCOL, BS, BS).astype(jnp.bfloat16)


def level_of(own_key, extent, cuts, least, top_value):
    def one(position, parts):
        heights = jax.random.uniform(jax.random.fold_in(jax.random.fold_in(own_key, 6), position), (parts,), jnp.float32, least / len(cuts), top_value / len(cuts))
        return jnp.repeat(jnp.exp(heights), extent[position] // parts).reshape((-1,) + (1,) * (len(extent) - position - 1))

    level = one(*cuts[0])
    for cut in cuts[1:]:
        level = level * one(*cut)
    return level


def gaussian(key, shape, scale, bound, pieces=(), kind=jnp.bfloat16):
    result = jax.random.normal(key, shape, jnp.float32) * scale
    if len(pieces) > 0:
        result = level_of(key, shape, pieces, -0.22, 0.18) * result
    return jnp.clip(result, min=-bound, max=bound).astype(kind)


def setup_inputs(seed: int = 0) -> dict:
    key_list = jax.random.split(jax.random.key(seed), 5)
    factor = draw_factor(jax.random.fold_in(key_list[4], 71), 0)
    right_side = gaussian(key_list[1], (NB // N_PCOL, N_PCOL, BS, NRHS), 1.0, 6.0, ((1, 32),))
    node_blocks = draw_node_blocks(jax.random.fold_in(key_list[4], 71), 0)
    front_mask = draw_front_mask(jax.random.fold_in(key_list[4], 71), 0)
    return {"factor": factor, "right_side": right_side, "node_blocks": node_blocks, "front_mask": front_mask}


def node_order():
    ordering = []
    for depth_now in range(LEVELS - 1, -1, -1):
        ordering.extend(range(2 ** depth_now - 1, 2 ** (depth_now + 1) - 1))
    return ordering


def node_table(node_blocks, total_blocks):
    node_count = node_blocks.shape[0]
    ordered = jnp.array(node_order(), dtype=jnp.int32)
    node_ids = jnp.arange(node_count, dtype=jnp.int32)
    pick_sizes = (ordered[:, None] == node_ids[None, :]).astype(jnp.int32)
    level_sizes = jnp.sum(pick_sizes * node_blocks[None, :], axis=1).astype(jnp.int32)
    block_ends = jnp.cumsum(level_sizes).astype(jnp.int32)
    block_ids = jnp.arange(total_blocks, dtype=jnp.int32)
    positions = jnp.sum((block_ids[:, None] >= block_ends[None, :]).astype(jnp.int32), axis=1).astype(jnp.int32)
    return jnp.sum((positions[:, None] == node_ids[None, :]).astype(jnp.int32) * ordered[None, :], axis=1).astype(jnp.int32)


def reference(factor, right_side, node_blocks, front_mask):
    blocks = factor.reshape(NB, NB, BS, BS)
    vectors = right_side.reshape(NB, BS, NRHS)
    block_node = node_table(node_blocks, NB)
    block_ids = jnp.arange(NB, dtype=jnp.int32)
    front_full = jnp.transpose(front_mask[block_node])
    diag_full = (block_node[:, None] == block_node[None, :]) & (block_ids[:, None] >= block_ids[None, :])
    solved = jnp.zeros((NB, BS, NRHS), jnp.bfloat16)
    for section_now in range(LEVELS):
        first_row = section_now * K
        after_row = first_row + K
        rows_now = jnp.arange(first_row, after_row, dtype=jnp.int32)
        if section_now == 0:
            rhs_now = vectors[first_row:after_row]
        else:
            earlier = solved[:first_row].reshape(section_now, K, BS, NRHS).astype(jnp.float32)

            def update_row(row_id):
                tile_set = blocks[row_id, :first_row].reshape(section_now, K, BS, BS).astype(jnp.float32)
                live_bits = front_full[row_id, :first_row].reshape(section_now, K).astype(jnp.float32)
                per_column = jnp.einsum("hcxy,hcyn->cxn", tile_set * live_bits[:, :, None, None], earlier, precision=lax.Precision.HIGHEST)
                rounded = lax.optimization_barrier(per_column.astype(jnp.bfloat16))
                return jnp.sum(rounded.astype(jnp.float32), axis=0)

            update = lax.map(update_row, rows_now)
            rhs_now = (vectors[first_row:after_row].astype(jnp.float32) - update).astype(jnp.bfloat16)
        rhs_float = rhs_now.astype(jnp.float32)

        def solve_row(row_id):
            tile_set = blocks[row_id, first_row:after_row].astype(jnp.float32)
            live_bits = diag_full[row_id, first_row:after_row].astype(jnp.float32)
            diag_terms = jnp.einsum("cxy,cyn->cxn", tile_set * live_bits[:, None, None], rhs_float, precision=lax.Precision.HIGHEST)
            rounded = lax.optimization_barrier(diag_terms.astype(jnp.bfloat16))
            return jnp.sum(rounded.astype(jnp.float32), axis=0).astype(jnp.bfloat16)

        solved = solved.at[first_row:after_row].set(lax.map(solve_row, rows_now))
    return solved.reshape(NB // N_PCOL, N_PCOL, BS, NRHS)
```

```python
import jax
import jax.numpy as jnp
from jax import lax
from jax.sharding import PartitionSpec as P

LEVELS = 4


def node_order():
    ordering = []
    for depth_now in range(LEVELS - 1, -1, -1):
        ordering.extend(range(2**depth_now - 1, 2 ** (depth_now + 1) - 1))
    return ordering


def node_table(node_blocks, total_blocks):
    node_count = node_blocks.shape[0]
    ordered = jnp.array(node_order(), dtype=jnp.int32)
    node_ids = jnp.arange(node_count, dtype=jnp.int32)
    pick_sizes = (ordered[:, None] == node_ids[None, :]).astype(jnp.int32)
    level_sizes = jnp.sum(pick_sizes * node_blocks[None, :], axis=1)
    block_ends = jnp.cumsum(level_sizes)
    block_ids = jnp.arange(total_blocks, dtype=jnp.int32)
    positions = jnp.sum((block_ids[:, None] >= block_ends[None, :]).astype(jnp.int32), axis=1)
    return jnp.sum(
        (positions[:, None] == node_ids[None, :]).astype(jnp.int32) * ordered[None, :], axis=1
    )


def lookup(values_table, indices):
    positions_all = jnp.arange(values_table.shape[0], dtype=jnp.int32)
    return jnp.sum(
        (indices[:, None] == positions_all[None, :]).astype(jnp.int32) * values_table[None, :],
        axis=1,
    )


def panel_products(tile_stack, live_bits, vector):
    products = jnp.einsum("nxy,yw->nxw", tile_stack, vector, preferred_element_type=jnp.float32)
    return products * live_bits.astype(jnp.float32)[:, None, None]


def local(factor, right_side, node_blocks, front_mask):
    rows_local = factor.shape[0]
    cols_local = factor.shape[2]
    block_size = factor.shape[4]
    prow_count = lax.axis_size("prow")
    pcol_count = lax.axis_size("pcol")
    prow_index = lax.axis_index("prow")
    pcol_index = lax.axis_index("pcol")
    total_blocks = rows_local * prow_count
    level_rows = pcol_count // prow_count
    piece_rows = block_size // pcol_count
    tile_grid = factor.reshape(rows_local, cols_local, block_size, block_size)
    columns_in = right_side.reshape(cols_local, block_size, right_side.shape[3])
    block_node = node_table(node_blocks, total_blocks)
    row_ids = jnp.arange(rows_local, dtype=jnp.int32) * prow_count + prow_index
    col_ids = jnp.arange(cols_local, dtype=jnp.int32) * pcol_count + pcol_index
    row_nodes = lookup(block_node, row_ids)
    col_nodes = lookup(block_node, col_ids)
    node_ids = jnp.arange(node_blocks.shape[0], dtype=jnp.int32)
    pick_node = (col_nodes[:, None] == node_ids[None, :]).astype(jnp.int32)
    front_rows = jnp.sum(pick_node[:, :, None] * front_mask[None, :, :], axis=1)
    block_all = jnp.arange(total_blocks, dtype=jnp.int32)
    pick_row = (row_ids[:, None] == block_all[None, :]).astype(jnp.int32)
    front_bits = jnp.sum(pick_row[:, None, :] * front_rows[None, :, :], axis=2)
    diag_bits = (
        (row_nodes[:, None] == col_nodes[None, :]) & (row_ids[:, None] >= col_ids[None, :])
    ).astype(jnp.int32)

    def reduce_route(level_terms):
        rhs_width = level_terms.shape[2]
        pieces = level_terms.astype(jnp.bfloat16).reshape(level_rows, pcol_count, piece_rows, rhs_width)
        pieces = jnp.transpose(pieces, (1, 0, 2, 3))
        got = lax.all_to_all(pieces, "pcol", 0, 0, tiled=True)
        summed = jnp.sum(got.astype(jnp.float32), axis=0).astype(jnp.bfloat16)
        spread = jnp.broadcast_to(summed[None], (prow_count,) + summed.shape)
        gathered = lax.all_to_all(spread, "prow", 0, 0, tiled=True)
        by_row = jnp.transpose(gathered, (1, 0, 2, 3)).reshape(pcol_count, piece_rows, rhs_width)
        arrived = lax.all_to_all(by_row, "pcol", 0, 0, tiled=True)
        return arrived.reshape(block_size, rhs_width)

    rhs_width = columns_in.shape[2]
    partial_value = jnp.zeros((rows_local, block_size, rhs_width), jnp.float32)
    solved_list = []
    for section_now in range(LEVELS):
        first_row = section_now * level_rows
        after_row = first_row + level_rows
        if section_now == 0:
            rhs_column = columns_in[0]
        else:
            update = reduce_route(partial_value[first_row:after_row]).astype(jnp.float32)
            rhs_column = (columns_in[section_now].astype(jnp.float32) - update).astype(jnp.bfloat16)
        diag_terms = panel_products(
            tile_grid[first_row:after_row, section_now],
            diag_bits[first_row:after_row, section_now],
            rhs_column,
        )
        solved = reduce_route(diag_terms)
        solved_list.append(solved)
        if section_now + 1 < LEVELS:
            update_terms = panel_products(
                tile_grid[after_row:, section_now], front_bits[after_row:, section_now], solved
            )
            partial_value = partial_value.at[after_row:].add(update_terms)
    solution = jnp.stack(solved_list)
    return solution.reshape(cols_local, 1, block_size, columns_in.shape[2])


def solution(mesh):
    in_specs = (P(None, "prow", None, "pcol", None, None), P(None, "pcol", None, None), P(), P())
    out_specs = P(None, "pcol", None, None)
    return jax.shard_map(local, mesh=mesh, in_specs=in_specs, out_specs=out_specs, check_vma=False)
```

```python
import jax
import jax.numpy as jnp
from jax import lax
from jax.sharding import PartitionSpec as P

LEVELS = 4


def node_order():
    ordering = []
    for depth_now in range(LEVELS - 1, -1, -1):
        ordering.extend(range(2**depth_now - 1, 2 ** (depth_now + 1) - 1))
    return ordering


def node_table(node_blocks, total_blocks):
    node_count = node_blocks.shape[0]
    ordered = jnp.array(node_order(), dtype=jnp.int32)
    node_ids = jnp.arange(node_count, dtype=jnp.int32)
    pick_sizes = (ordered[:, None] == node_ids[None, :]).astype(jnp.int32)
    level_sizes = jnp.sum(pick_sizes * node_blocks[None, :], axis=1)
    block_ends = jnp.cumsum(level_sizes)
    block_ids = jnp.arange(total_blocks, dtype=jnp.int32)
    positions = jnp.sum((block_ids[:, None] >= block_ends[None, :]).astype(jnp.int32), axis=1)
    return jnp.sum(
        (positions[:, None] == node_ids[None, :]).astype(jnp.int32) * ordered[None, :], axis=1
    )


def lookup(values_table, indices):
    positions_all = jnp.arange(values_table.shape[0], dtype=jnp.int32)
    return jnp.sum(
        (indices[:, None] == positions_all[None, :]).astype(jnp.int32) * values_table[None, :],
        axis=1,
    )


def panel_products(tile_stack, live_bits, vector):
    products = jnp.einsum("nxy,yw->nxw", tile_stack, vector, preferred_element_type=jnp.float32)
    return products * live_bits.astype(jnp.float32)[:, None, None]


def local(factor, right_side, node_blocks, front_mask):
    rows_local = factor.shape[0]
    cols_local = factor.shape[2]
    block_size = factor.shape[4]
    prow_count = lax.axis_size("prow")
    pcol_count = lax.axis_size("pcol")
    prow_index = lax.axis_index("prow")
    pcol_index = lax.axis_index("pcol")
    total_blocks = rows_local * prow_count
    level_rows = pcol_count // prow_count
    piece_rows = block_size // pcol_count
    prow_piece = block_size // prow_count
    tile_grid = factor.reshape(rows_local, cols_local, block_size, block_size)
    columns_in = right_side.reshape(cols_local, block_size, right_side.shape[3])
    rhs_width = columns_in.shape[2]
    block_node = node_table(node_blocks, total_blocks)
    row_ids = jnp.arange(rows_local, dtype=jnp.int32) * prow_count + prow_index
    col_ids = jnp.arange(cols_local, dtype=jnp.int32) * pcol_count + pcol_index
    row_nodes = lookup(block_node, row_ids)
    col_nodes = lookup(block_node, col_ids)
    node_ids = jnp.arange(node_blocks.shape[0], dtype=jnp.int32)
    pick_node = (col_nodes[:, None] == node_ids[None, :]).astype(jnp.int32)
    front_rows = jnp.sum(pick_node[:, :, None] * front_mask[None, :, :], axis=1)
    block_all = jnp.arange(total_blocks, dtype=jnp.int32)
    pick_row = (row_ids[:, None] == block_all[None, :]).astype(jnp.int32)
    front_bits = jnp.sum(pick_row[:, None, :] * front_rows[None, :, :], axis=2)
    diag_bits = (
        (row_nodes[:, None] == col_nodes[None, :]) & (row_ids[:, None] >= col_ids[None, :])
    ).astype(jnp.int32)

    level_groups = level_rows
    group_of_col = pcol_index // prow_count
    shifted = []
    for shift in range(level_groups):
        pick_k = (group_of_col + shift) % level_groups
        sent = jnp.stack(
            [
                lax.dynamic_index_in_dim(tile_grid[:, level], level * level_groups + pick_k, 0, False)
                for level in range(1, LEVELS)
            ]
        )
        pairs = []
        for p_src in range(prow_count):
            for c_src in range(pcol_count):
                k_dst = (c_src // prow_count + shift) % level_groups
                dst = (c_src % prow_count) * pcol_count + k_dst * prow_count + p_src
                pairs.append((p_src * pcol_count + c_src, dst))
        shifted.append(lax.ppermute(sent, ("prow", "pcol"), pairs))
    shifted = jnp.stack(shifted)
    diag_tiles = jnp.stack(
        [
            lax.dynamic_index_in_dim(shifted, (group_of_col - m) % level_groups, 0, False)
            for m in range(level_groups)
        ],
        axis=1,
    )
    own_row = jnp.arange(1, LEVELS, dtype=jnp.int32)[:, None] * pcol_count + pcol_index
    group_cols = (
        jnp.arange(1, LEVELS, dtype=jnp.int32)[:, None] * pcol_count
        + prow_index
        + prow_count * jnp.arange(level_groups, dtype=jnp.int32)[None, :]
    )
    own_node = lookup(block_node, own_row.reshape(-1)).reshape(own_row.shape)
    group_node = lookup(block_node, group_cols.reshape(-1)).reshape(group_cols.shape)
    group_bits = ((own_node == group_node) & (own_row >= group_cols)).astype(jnp.float32)

    def reduce_route(level_terms):
        pieces = level_terms.astype(jnp.bfloat16).reshape(level_rows, pcol_count, piece_rows, rhs_width)
        pieces = jnp.transpose(pieces, (1, 0, 2, 3))
        got = lax.all_to_all(pieces, "pcol", 0, 0, tiled=True)
        summed = jnp.sum(got.astype(jnp.float32), axis=0).astype(jnp.bfloat16)
        spread = jnp.broadcast_to(summed[None], (prow_count,) + summed.shape)
        gathered = lax.all_to_all(spread, "prow", 0, 0, tiled=True)
        by_row = jnp.transpose(gathered, (1, 0, 2, 3)).reshape(pcol_count, piece_rows, rhs_width)
        arrived = lax.all_to_all(by_row, "pcol", 0, 0, tiled=True)
        return arrived.reshape(block_size, rhs_width)

    def reduce_gather_pcol(level_terms):
        pieces = level_terms.astype(jnp.bfloat16).reshape(level_rows, pcol_count, piece_rows, rhs_width)
        pieces = jnp.transpose(pieces, (1, 0, 2, 3))
        got = lax.all_to_all(pieces, "pcol", 0, 0, tiled=True)
        summed = (-jnp.sum(got.astype(jnp.float32), axis=0)).astype(jnp.bfloat16)
        spread = jnp.broadcast_to(summed[None], (pcol_count,) + summed.shape)
        gathered = lax.all_to_all(spread, "pcol", 0, 0, tiled=True)
        return jnp.transpose(gathered, (1, 0, 2, 3)).reshape(level_rows, block_size, rhs_width)

    def reduce_gather_prow(row_terms):
        pieces = row_terms.astype(jnp.bfloat16).reshape(prow_count, prow_piece, rhs_width)
        got = lax.all_to_all(pieces, "prow", 0, 0, tiled=True)
        summed = jnp.sum(got.astype(jnp.float32), axis=0).astype(jnp.bfloat16)
        spread = jnp.broadcast_to(summed[None], (prow_count,) + summed.shape)
        gathered = lax.all_to_all(spread, "prow", 0, 0, tiled=True)
        return gathered.reshape(block_size, rhs_width)

    row_in_group = prow_index + prow_count * jnp.arange(level_rows, dtype=jnp.int32)
    owns_row = (row_in_group == pcol_index).astype(jnp.float32)

    partial_value = jnp.zeros((rows_local, block_size, rhs_width), jnp.float32)
    solved_list = []
    for section_now in range(LEVELS):
        first_row = section_now * level_rows
        after_row = first_row + level_rows
        if section_now == 0:
            diag_terms = panel_products(
                tile_grid[first_row:after_row, 0], diag_bits[first_row:after_row, 0], columns_in[0]
            )
            solved = reduce_route(diag_terms)
        else:
            own_b = columns_in[section_now].astype(jnp.float32)
            contrib = partial_value[first_row:after_row] - owns_row[:, None, None] * own_b[None]
            rhs_group = reduce_gather_pcol(contrib)
            tiles = diag_tiles[section_now - 1] * group_bits[section_now - 1][:, None, None].astype(
                jnp.bfloat16
            )
            row_terms = jnp.einsum(
                "mxy,myw->xw", tiles, rhs_group, preferred_element_type=jnp.float32
            )
            solved = reduce_gather_prow(row_terms)
        solved_list.append(solved)
        if section_now + 1 < LEVELS:
            update_terms = panel_products(
                tile_grid[after_row:, section_now], front_bits[after_row:, section_now], solved
            )
            partial_value = partial_value.at[after_row:].add(update_terms)
    solution = jnp.stack(solved_list)
    return solution.reshape(cols_local, 1, block_size, columns_in.shape[2])


def solution(mesh):
    in_specs = (P(None, "prow", None, "pcol", None, None), P(None, "pcol", None, None), P(), P())
    out_specs = P(None, "pcol", None, None)
    return jax.shard_map(local, mesh=mesh, in_specs=in_specs, out_specs=out_specs, check_vma=False)
```

```python
import jax
import jax.numpy as jnp
from jax import lax
from jax.sharding import PartitionSpec as P

LEVELS = 4


def node_order():
    ordering = []
    for depth_now in range(LEVELS - 1, -1, -1):
        ordering.extend(range(2**depth_now - 1, 2 ** (depth_now + 1) - 1))
    return ordering


def node_table(node_blocks, total_blocks):
    node_count = node_blocks.shape[0]
    ordered = jnp.array(node_order(), dtype=jnp.int32)
    node_ids = jnp.arange(node_count, dtype=jnp.int32)
    pick_sizes = (ordered[:, None] == node_ids[None, :]).astype(jnp.int32)
    level_sizes = jnp.sum(pick_sizes * node_blocks[None, :], axis=1)
    block_ends = jnp.cumsum(level_sizes)
    block_ids = jnp.arange(total_blocks, dtype=jnp.int32)
    positions = jnp.sum((block_ids[:, None] >= block_ends[None, :]).astype(jnp.int32), axis=1)
    return jnp.sum(
        (positions[:, None] == node_ids[None, :]).astype(jnp.int32) * ordered[None, :], axis=1
    )


def lookup(values_table, indices):
    positions_all = jnp.arange(values_table.shape[0], dtype=jnp.int32)
    return jnp.sum(
        (indices[:, None] == positions_all[None, :]).astype(jnp.int32) * values_table[None, :],
        axis=1,
    )


def panel_products(tile_stack, live_bits, vector):
    products = jnp.stack(
        [jnp.dot(tile_stack[n], vector, preferred_element_type=jnp.float32) for n in range(tile_stack.shape[0])]
    )
    return products * live_bits.astype(jnp.float32)[:, None, None]


def local(factor, right_side, node_blocks, front_mask):
    rows_local = factor.shape[0]
    cols_local = factor.shape[2]
    block_size = factor.shape[4]
    prow_count = lax.axis_size("prow")
    pcol_count = lax.axis_size("pcol")
    prow_index = lax.axis_index("prow")
    pcol_index = lax.axis_index("pcol")
    total_blocks = rows_local * prow_count
    level_rows = pcol_count // prow_count
    piece_rows = block_size // pcol_count
    prow_piece = block_size // prow_count
    tile_grid = factor.reshape(rows_local, cols_local, block_size, block_size)
    columns_in = right_side.reshape(cols_local, block_size, right_side.shape[3])
    rhs_width = columns_in.shape[2]
    block_node = node_table(node_blocks, total_blocks)
    row_ids = jnp.arange(rows_local, dtype=jnp.int32) * prow_count + prow_index
    col_ids = jnp.arange(cols_local, dtype=jnp.int32) * pcol_count + pcol_index
    row_nodes = lookup(block_node, row_ids)
    col_nodes = lookup(block_node, col_ids)
    node_ids = jnp.arange(node_blocks.shape[0], dtype=jnp.int32)
    pick_node = (col_nodes[:, None] == node_ids[None, :]).astype(jnp.int32)
    front_rows = jnp.sum(pick_node[:, :, None] * front_mask[None, :, :], axis=1)
    block_all = jnp.arange(total_blocks, dtype=jnp.int32)
    pick_row = (row_ids[:, None] == block_all[None, :]).astype(jnp.int32)
    front_bits = jnp.sum(pick_row[:, None, :] * front_rows[None, :, :], axis=2)
    diag_bits = (
        (row_nodes[:, None] == col_nodes[None, :]) & (row_ids[:, None] >= col_ids[None, :])
    ).astype(jnp.int32)

    level_groups = level_rows
    group_of_col = pcol_index // prow_count
    shifted = []
    for shift in range(level_groups):
        pick_k = (group_of_col + shift) % level_groups
        sent = jnp.stack(
            [
                lax.dynamic_index_in_dim(tile_grid[:, level], level * level_groups + pick_k, 0, False)
                for level in range(1, LEVELS)
            ]
        )
        pairs = []
        for p_src in range(prow_count):
            for c_src in range(pcol_count):
                k_dst = (c_src // prow_count + shift) % level_groups
                if c_src > k_dst * prow_count + p_src:
                    continue
                dst = (c_src % prow_count) * pcol_count + k_dst * prow_count + p_src
                pairs.append((p_src * pcol_count + c_src, dst))
        shifted.append(lax.ppermute(sent, ("prow", "pcol"), pairs))
    shifted = jnp.stack(shifted)
    diag_tiles = jnp.stack(
        [
            lax.dynamic_index_in_dim(shifted, (group_of_col - m) % level_groups, 0, False)
            for m in range(level_groups)
        ],
        axis=1,
    )
    own_row = jnp.arange(1, LEVELS, dtype=jnp.int32)[:, None] * pcol_count + pcol_index
    group_cols = (
        jnp.arange(1, LEVELS, dtype=jnp.int32)[:, None] * pcol_count
        + prow_index
        + prow_count * jnp.arange(level_groups, dtype=jnp.int32)[None, :]
    )
    own_node = lookup(block_node, own_row.reshape(-1)).reshape(own_row.shape)
    group_node = lookup(block_node, group_cols.reshape(-1)).reshape(group_cols.shape)
    group_bits = ((own_node == group_node) & (own_row >= group_cols)).astype(jnp.float32)

    def reduce_route(level_terms):
        pieces = level_terms.astype(jnp.bfloat16).reshape(level_rows, pcol_count, piece_rows, rhs_width)
        pieces = jnp.transpose(pieces, (1, 0, 2, 3))
        got = lax.all_to_all(pieces, "pcol", 0, 0, tiled=True)
        summed = jnp.sum(got.astype(jnp.float32), axis=0).astype(jnp.bfloat16)
        spread = jnp.broadcast_to(summed[None], (prow_count,) + summed.shape)
        gathered = lax.all_to_all(spread, "prow", 0, 0, tiled=True)
        by_row = jnp.transpose(gathered, (1, 0, 2, 3)).reshape(pcol_count, piece_rows, rhs_width)
        arrived = lax.all_to_all(by_row, "pcol", 0, 0, tiled=True)
        return arrived.reshape(block_size, rhs_width)

    def reduce_gather_pcol(level_terms):
        pieces = level_terms.astype(jnp.bfloat16).reshape(level_rows, pcol_count, piece_rows, rhs_width)
        pieces = jnp.transpose(pieces, (1, 0, 2, 3))
        got = lax.all_to_all(pieces, "pcol", 0, 0, tiled=True)
        summed = (-jnp.sum(got.astype(jnp.float32), axis=0)).astype(jnp.bfloat16)
        spread = jnp.broadcast_to(summed[None], (pcol_count,) + summed.shape)
        gathered = lax.all_to_all(spread, "pcol", 0, 0, tiled=True)
        return jnp.transpose(gathered, (1, 0, 2, 3)).reshape(level_rows, block_size, rhs_width)

    def reduce_gather_prow(row_terms):
        pieces = row_terms.astype(jnp.bfloat16).reshape(prow_count, prow_piece, rhs_width)
        got = lax.all_to_all(pieces, "prow", 0, 0, tiled=True)
        summed = jnp.sum(got.astype(jnp.float32), axis=0).astype(jnp.bfloat16)
        spread = jnp.broadcast_to(summed[None], (prow_count,) + summed.shape)
        gathered = lax.all_to_all(spread, "prow", 0, 0, tiled=True)
        return gathered.reshape(block_size, rhs_width)

    row_in_group = prow_index + prow_count * jnp.arange(level_rows, dtype=jnp.int32)
    owns_row = (row_in_group == pcol_index).astype(jnp.float32)

    partial_value = jnp.zeros((rows_local, block_size, rhs_width), jnp.float32)
    solved_list = []
    for section_now in range(LEVELS):
        first_row = section_now * level_rows
        after_row = first_row + level_rows
        if section_now == 0:
            diag_terms = panel_products(
                tile_grid[first_row:after_row, 0], diag_bits[first_row:after_row, 0], columns_in[0]
            )
            solved = reduce_route(diag_terms)
        else:
            own_b = columns_in[section_now].astype(jnp.float32)
            contrib = partial_value[first_row:after_row] - owns_row[:, None, None] * own_b[None]
            rhs_group = reduce_gather_pcol(contrib)
            tiles = diag_tiles[section_now - 1] * group_bits[section_now - 1][:, None, None].astype(
                jnp.bfloat16
            )
            row_terms = jnp.einsum(
                "mxy,myw->xw", tiles, rhs_group, preferred_element_type=jnp.float32
            )
            solved = reduce_gather_prow(row_terms)
        solved_list.append(solved)
        if section_now + 1 < LEVELS:
            update_terms = panel_products(
                tile_grid[after_row:, section_now], front_bits[after_row:, section_now], solved
            )
            partial_value = partial_value.at[after_row:].add(update_terms)
    solution = jnp.stack(solved_list)
    return solution.reshape(cols_local, 1, block_size, columns_in.shape[2])


def solution(mesh):
    in_specs = (P(None, "prow", None, "pcol", None, None), P(None, "pcol", None, None), P(), P())
    out_specs = P(None, "pcol", None, None)
    return jax.shard_map(local, mesh=mesh, in_specs=in_specs, out_specs=out_specs, check_vma=False)
```

```python
import jax
import jax.numpy as jnp
from jax import lax
from jax.sharding import PartitionSpec as P

LEVELS = 4


def node_order():
    ordering = []
    for depth_now in range(LEVELS - 1, -1, -1):
        ordering.extend(range(2**depth_now - 1, 2 ** (depth_now + 1) - 1))
    return ordering


def node_table(node_blocks, total_blocks):
    node_count = node_blocks.shape[0]
    ordered = jnp.array(node_order(), dtype=jnp.int32)
    node_ids = jnp.arange(node_count, dtype=jnp.int32)
    pick_sizes = (ordered[:, None] == node_ids[None, :]).astype(jnp.int32)
    level_sizes = jnp.sum(pick_sizes * node_blocks[None, :], axis=1)
    block_ends = jnp.cumsum(level_sizes)
    block_ids = jnp.arange(total_blocks, dtype=jnp.int32)
    positions = jnp.sum((block_ids[:, None] >= block_ends[None, :]).astype(jnp.int32), axis=1)
    return jnp.sum(
        (positions[:, None] == node_ids[None, :]).astype(jnp.int32) * ordered[None, :], axis=1
    )


def lookup(values_table, indices):
    positions_all = jnp.arange(values_table.shape[0], dtype=jnp.int32)
    return jnp.sum(
        (indices[:, None] == positions_all[None, :]).astype(jnp.int32) * values_table[None, :],
        axis=1,
    )


def panel_products(tile_stack, live_bits, vector):
    products = jnp.einsum("nxy,yw->nxw", tile_stack, vector, preferred_element_type=jnp.float32)
    return products * live_bits.astype(jnp.float32)[:, None, None]


def local(factor, right_side, node_blocks, front_mask):
    rows_local = factor.shape[0]
    cols_local = factor.shape[2]
    block_size = factor.shape[4]
    prow_count = lax.axis_size("prow")
    pcol_count = lax.axis_size("pcol")
    prow_index = lax.axis_index("prow")
    pcol_index = lax.axis_index("pcol")
    total_blocks = rows_local * prow_count
    level_rows = pcol_count // prow_count
    piece_rows = block_size // pcol_count
    tile_grid = factor.reshape(rows_local, cols_local, block_size, block_size)
    tile_rows = factor.reshape(rows_local, cols_local * block_size, block_size)

    def column_tiles(first, col):
        return tile_rows[first:, col * block_size:(col + 1) * block_size]
    columns_in = right_side.reshape(cols_local, block_size, right_side.shape[3])
    block_node = node_table(node_blocks, total_blocks)
    row_ids = jnp.arange(rows_local, dtype=jnp.int32) * prow_count + prow_index
    col_ids = jnp.arange(cols_local, dtype=jnp.int32) * pcol_count + pcol_index
    row_nodes = lookup(block_node, row_ids)
    col_nodes = lookup(block_node, col_ids)
    node_ids = jnp.arange(node_blocks.shape[0], dtype=jnp.int32)
    pick_node = (col_nodes[:, None] == node_ids[None, :]).astype(jnp.int32)
    front_rows = jnp.sum(pick_node[:, :, None] * front_mask[None, :, :], axis=1)
    block_all = jnp.arange(total_blocks, dtype=jnp.int32)
    pick_row = (row_ids[:, None] == block_all[None, :]).astype(jnp.int32)
    front_bits = jnp.sum(pick_row[:, None, :] * front_rows[None, :, :], axis=2)
    diag_bits = (
        (row_nodes[:, None] == col_nodes[None, :]) & (row_ids[:, None] >= col_ids[None, :])
    ).astype(jnp.int32)

    def reduce_route(level_terms):
        rhs_width = level_terms.shape[2]
        pieces = level_terms.astype(jnp.bfloat16).reshape(level_rows, pcol_count, piece_rows, rhs_width)
        pieces = jnp.transpose(pieces, (1, 0, 2, 3))
        got = lax.all_to_all(pieces, "pcol", 0, 0, tiled=True)
        summed = jnp.sum(got.astype(jnp.float32), axis=0).astype(jnp.bfloat16)
        spread = jnp.broadcast_to(summed[None], (prow_count,) + summed.shape)
        gathered = lax.all_to_all(spread, "prow", 0, 0, tiled=True)
        by_row = jnp.transpose(gathered, (1, 0, 2, 3)).reshape(pcol_count, piece_rows, rhs_width)
        arrived = lax.all_to_all(by_row, "pcol", 0, 0, tiled=True)
        return arrived.reshape(block_size, rhs_width)

    rhs_width = columns_in.shape[2]
    partial_value = jnp.zeros((rows_local, block_size, rhs_width), jnp.float32)
    solved_list = []
    for section_now in range(LEVELS):
        first_row = section_now * level_rows
        after_row = first_row + level_rows
        if section_now == 0:
            rhs_column = columns_in[0]
        else:
            update = reduce_route(partial_value[first_row:after_row]).astype(jnp.float32)
            rhs_column = (columns_in[section_now].astype(jnp.float32) - update).astype(jnp.bfloat16)
        diag_terms = panel_products(
            column_tiles(first_row, section_now)[:level_rows],
            diag_bits[first_row:after_row, section_now],
            rhs_column,
        )
        solved = reduce_route(diag_terms)
        solved_list.append(solved)
        if section_now + 1 < LEVELS:
            update_terms = panel_products(
                column_tiles(after_row, section_now), front_bits[after_row:, section_now], solved
            )
            partial_value = partial_value.at[after_row:].add(update_terms)
    solution = jnp.stack(solved_list)
    return solution.reshape(cols_local, 1, block_size, columns_in.shape[2])


def solution(mesh):
    in_specs = (P(None, "prow", None, "pcol", None, None), P(None, "pcol", None, None), P(), P())
    out_specs = P(None, "pcol", None, None)
    return jax.shard_map(local, mesh=mesh, in_specs=in_specs, out_specs=out_specs, check_vma=False)
```

```python
import jax
import jax.numpy as jnp
from jax import lax
from jax.sharding import PartitionSpec as P

LEVELS = 4


def node_order():
    ordering = []
    for depth_now in range(LEVELS - 1, -1, -1):
        ordering.extend(range(2**depth_now - 1, 2 ** (depth_now + 1) - 1))
    return ordering


def node_table(node_blocks, total_blocks):
    node_count = node_blocks.shape[0]
    ordered = jnp.array(node_order(), dtype=jnp.int32)
    node_ids = jnp.arange(node_count, dtype=jnp.int32)
    pick_sizes = (ordered[:, None] == node_ids[None, :]).astype(jnp.int32)
    level_sizes = jnp.sum(pick_sizes * node_blocks[None, :], axis=1)
    block_ends = jnp.cumsum(level_sizes)
    block_ids = jnp.arange(total_blocks, dtype=jnp.int32)
    positions = jnp.sum((block_ids[:, None] >= block_ends[None, :]).astype(jnp.int32), axis=1)
    return jnp.sum(
        (positions[:, None] == node_ids[None, :]).astype(jnp.int32) * ordered[None, :], axis=1
    )


def lookup(values_table, indices):
    positions_all = jnp.arange(values_table.shape[0], dtype=jnp.int32)
    return jnp.sum(
        (indices[:, None] == positions_all[None, :]).astype(jnp.int32) * values_table[None, :],
        axis=1,
    )


def panel_products(tile_stack, live_bits, vector):
    products = jnp.einsum("nxy,yw->nxw", tile_stack, vector, preferred_element_type=jnp.float32)
    return products * live_bits.astype(jnp.float32)[:, None, None]


def local(factor, right_side, node_blocks, front_mask):
    rows_local = factor.shape[0]
    cols_local = factor.shape[2]
    block_size = factor.shape[4]
    prow_count = lax.axis_size("prow")
    pcol_count = lax.axis_size("pcol")
    prow_index = lax.axis_index("prow")
    pcol_index = lax.axis_index("pcol")
    total_blocks = rows_local * prow_count
    level_rows = pcol_count // prow_count
    piece_rows = block_size // pcol_count
    prow_piece = block_size // prow_count
    tile_grid = factor.reshape(rows_local, cols_local, block_size, block_size)
    tile_rows = factor.reshape(rows_local, cols_local * block_size, block_size)

    def column_tiles(first, col):
        return tile_rows[first:, col * block_size:(col + 1) * block_size]
    columns_in = right_side.reshape(cols_local, block_size, right_side.shape[3])
    rhs_width = columns_in.shape[2]
    block_node = node_table(node_blocks, total_blocks)
    row_ids = jnp.arange(rows_local, dtype=jnp.int32) * prow_count + prow_index
    col_ids = jnp.arange(cols_local, dtype=jnp.int32) * pcol_count + pcol_index
    row_nodes = lookup(block_node, row_ids)
    col_nodes = lookup(block_node, col_ids)
    node_ids = jnp.arange(node_blocks.shape[0], dtype=jnp.int32)
    pick_node = (col_nodes[:, None] == node_ids[None, :]).astype(jnp.int32)
    front_rows = jnp.sum(pick_node[:, :, None] * front_mask[None, :, :], axis=1)
    block_all = jnp.arange(total_blocks, dtype=jnp.int32)
    pick_row = (row_ids[:, None] == block_all[None, :]).astype(jnp.int32)
    front_bits = jnp.sum(pick_row[:, None, :] * front_rows[None, :, :], axis=2)
    diag_bits = (
        (row_nodes[:, None] == col_nodes[None, :]) & (row_ids[:, None] >= col_ids[None, :])
    ).astype(jnp.int32)

    level_groups = level_rows
    group_of_col = pcol_index // prow_count
    shifted = []
    for shift in range(level_groups):
        pick_k = (group_of_col + shift) % level_groups
        sent = jnp.stack(
            [
                lax.dynamic_index_in_dim(tile_grid[:, level], level * level_groups + pick_k, 0, False)
                for level in range(LEVELS)
            ]
            + [columns_in[0]]
        )
        pairs = []
        for p_src in range(prow_count):
            for c_src in range(pcol_count):
                k_dst = (c_src // prow_count + shift) % level_groups
                if c_src > k_dst * prow_count + p_src:
                    continue
                dst = (c_src % prow_count) * pcol_count + k_dst * prow_count + p_src
                pairs.append((p_src * pcol_count + c_src, dst))
        shifted.append(lax.ppermute(sent, ("prow", "pcol"), pairs))
    shifted = jnp.stack(shifted)
    diag_tiles = jnp.stack(
        [
            lax.dynamic_index_in_dim(shifted, (group_of_col - m) % level_groups, 0, False)
            for m in range(level_groups)
        ],
        axis=1,
    )
    own_row = jnp.arange(LEVELS, dtype=jnp.int32)[:, None] * pcol_count + pcol_index
    group_cols = (
        jnp.arange(LEVELS, dtype=jnp.int32)[:, None] * pcol_count
        + prow_index
        + prow_count * jnp.arange(level_groups, dtype=jnp.int32)[None, :]
    )
    own_node = lookup(block_node, own_row.reshape(-1)).reshape(own_row.shape)
    group_node = lookup(block_node, group_cols.reshape(-1)).reshape(group_cols.shape)
    group_bits = ((own_node == group_node) & (own_row >= group_cols)).astype(jnp.float32)

    def reduce_gather_pcol(level_terms):
        pieces = level_terms.astype(jnp.bfloat16).reshape(level_rows, pcol_count, piece_rows, rhs_width)
        pieces = jnp.transpose(pieces, (1, 0, 2, 3))
        got = lax.all_to_all(pieces, "pcol", 0, 0, tiled=True)
        summed = (-jnp.sum(got.astype(jnp.float32), axis=0)).astype(jnp.bfloat16)
        spread = jnp.broadcast_to(summed[None], (pcol_count,) + summed.shape)
        gathered = lax.all_to_all(spread, "pcol", 0, 0, tiled=True)
        return jnp.transpose(gathered, (1, 0, 2, 3)).reshape(level_rows, block_size, rhs_width)

    def reduce_gather_prow(row_terms):
        pieces = row_terms.astype(jnp.bfloat16).reshape(prow_count, prow_piece, rhs_width)
        got = lax.all_to_all(pieces, "prow", 0, 0, tiled=True)
        summed = jnp.sum(got.astype(jnp.float32), axis=0).astype(jnp.bfloat16)
        spread = jnp.broadcast_to(summed[None], (prow_count,) + summed.shape)
        gathered = lax.all_to_all(spread, "prow", 0, 0, tiled=True)
        return gathered.reshape(block_size, rhs_width)

    row_in_group = prow_index + prow_count * jnp.arange(level_rows, dtype=jnp.int32)
    owns_row = (row_in_group == pcol_index).astype(jnp.float32)

    partial_value = jnp.zeros((rows_local, block_size, rhs_width), jnp.float32)
    solved_list = []
    for section_now in range(LEVELS):
        first_row = section_now * level_rows
        after_row = first_row + level_rows
        if section_now == 0:
            rhs_group = diag_tiles[LEVELS]
        else:
            own_b = columns_in[section_now].astype(jnp.float32)
            contrib = partial_value[first_row:after_row] - owns_row[:, None, None] * own_b[None]
            rhs_group = reduce_gather_pcol(contrib)
        tiles = diag_tiles[section_now] * group_bits[section_now][:, None, None].astype(jnp.bfloat16)
        row_terms = jnp.einsum("mxy,myw->xw", tiles, rhs_group, preferred_element_type=jnp.float32)
        solved = reduce_gather_prow(row_terms)
        solved_list.append(solved)
        if section_now + 1 < LEVELS:
            update_terms = panel_products(
                column_tiles(after_row, section_now), front_bits[after_row:, section_now], solved
            )
            partial_value = partial_value.at[after_row:].add(update_terms)
    solution = jnp.stack(solved_list)
    return solution.reshape(cols_local, 1, block_size, columns_in.shape[2])


def solution(mesh):
    in_specs = (P(None, "prow", None, "pcol", None, None), P(None, "pcol", None, None), P(), P())
    out_specs = P(None, "pcol", None, None)
    return jax.shard_map(local, mesh=mesh, in_specs=in_specs, out_specs=out_specs, check_vma=False)
```

```python
import jax
import jax.numpy as jnp
from jax import lax
from jax.sharding import PartitionSpec as P

LEVELS = 4
PROW = ("x", "core")
PCOL = ("y", "z")
RING = "z"


def node_order():
    ordering = []
    for depth_now in range(LEVELS - 1, -1, -1):
        ordering.extend(range(2**depth_now - 1, 2 ** (depth_now + 1) - 1))
    return ordering


def node_table(node_blocks, total_blocks):
    node_count = node_blocks.shape[0]
    ordered = jnp.array(node_order(), dtype=jnp.int32)
    node_ids = jnp.arange(node_count, dtype=jnp.int32)
    pick_sizes = (ordered[:, None] == node_ids[None, :]).astype(jnp.int32)
    level_sizes = jnp.sum(pick_sizes * node_blocks[None, :], axis=1)
    block_ends = jnp.cumsum(level_sizes)
    block_ids = jnp.arange(total_blocks, dtype=jnp.int32)
    positions = jnp.sum((block_ids[:, None] >= block_ends[None, :]).astype(jnp.int32), axis=1)
    return jnp.sum(
        (positions[:, None] == node_ids[None, :]).astype(jnp.int32) * ordered[None, :], axis=1
    )


def lookup(values_table, indices):
    positions_all = jnp.arange(values_table.shape[0], dtype=jnp.int32)
    return jnp.sum(
        (indices[:, None] == positions_all[None, :]).astype(jnp.int32) * values_table[None, :],
        axis=1,
    )


def panel_products(tile_stack, live_bits, vector):
    products = jnp.einsum("nxy,yw->nxw", tile_stack, vector, preferred_element_type=jnp.float32)
    return products * live_bits.astype(jnp.float32)[:, None, None]


def local(factor, right_side, node_blocks, front_mask):
    rows_local = factor.shape[0]
    cols_local = factor.shape[2]
    block_size = factor.shape[4]
    prow_count = lax.axis_size(PROW)
    pcol_count = lax.axis_size(PCOL)
    prow_index = lax.axis_index(PROW)
    pcol_index = lax.axis_index(PCOL)
    ring = lax.axis_size(RING)
    chunk_rows = block_size // ring
    total_blocks = rows_local * prow_count
    level_rows = pcol_count // prow_count
    piece_rows = block_size // pcol_count
    tile_grid = factor.reshape(rows_local, cols_local, block_size, block_size)
    tile_rows = factor.reshape(rows_local, cols_local * block_size, block_size)

    def column_tiles(first, col):
        return tile_rows[first:, col * block_size:(col + 1) * block_size]
    columns_in = right_side.reshape(cols_local, block_size, right_side.shape[3])
    block_node = node_table(node_blocks, total_blocks)
    row_ids = jnp.arange(rows_local, dtype=jnp.int32) * prow_count + prow_index
    col_ids = jnp.arange(cols_local, dtype=jnp.int32) * pcol_count + pcol_index
    row_nodes = lookup(block_node, row_ids)
    col_nodes = lookup(block_node, col_ids)
    node_ids = jnp.arange(node_blocks.shape[0], dtype=jnp.int32)
    pick_node = (col_nodes[:, None] == node_ids[None, :]).astype(jnp.int32)
    front_rows = jnp.sum(pick_node[:, :, None] * front_mask[None, :, :], axis=1)
    block_all = jnp.arange(total_blocks, dtype=jnp.int32)
    pick_row = (row_ids[:, None] == block_all[None, :]).astype(jnp.int32)
    front_bits = jnp.sum(pick_row[:, None, :] * front_rows[None, :, :], axis=2)
    diag_bits = (
        (row_nodes[:, None] == col_nodes[None, :]) & (row_ids[:, None] >= col_ids[None, :])
    ).astype(jnp.int32)

    def reduce_route(level_terms):
        rhs_width = level_terms.shape[2]
        pieces = level_terms.astype(jnp.bfloat16).reshape(pcol_count, chunk_rows, rhs_width)
        got = lax.all_to_all(pieces, PCOL, 0, 0, tiled=True)
        summed = jnp.sum(got.astype(jnp.float32), axis=0).astype(jnp.bfloat16)
        spread = jnp.broadcast_to(summed[None], (prow_count,) + summed.shape)
        gathered = lax.all_to_all(spread, PROW, 0, 0, tiled=True)
        arrived = lax.all_to_all(gathered, RING, 0, 0, tiled=True)
        return arrived.reshape(block_size, rhs_width)

    rhs_width = columns_in.shape[2]
    partial_value = jnp.zeros((rows_local, block_size, rhs_width), jnp.float32)
    solved_list = []
    for section_now in range(LEVELS):
        first_row = section_now * level_rows
        after_row = first_row + level_rows
        if section_now == 0:
            rhs_column = columns_in[0]
        else:
            update = reduce_route(partial_value[first_row:after_row]).astype(jnp.float32)
            rhs_column = (columns_in[section_now].astype(jnp.float32) - update).astype(jnp.bfloat16)
        diag_terms = panel_products(
            column_tiles(first_row, section_now)[:level_rows],
            diag_bits[first_row:after_row, section_now],
            rhs_column,
        )
        solved = reduce_route(diag_terms)
        solved_list.append(solved)
        if section_now + 1 < LEVELS:
            update_terms = panel_products(
                column_tiles(after_row, section_now), front_bits[after_row:, section_now], solved
            )
            partial_value = partial_value.at[after_row:].add(update_terms)
    solution = jnp.stack(solved_list)
    return solution.reshape(cols_local, 1, block_size, columns_in.shape[2])


def solution(mesh):
    fine = jax.sharding.Mesh(
        mesh.devices.reshape(4, mesh.devices.shape[0] // 4, 4, mesh.devices.shape[1] // 4), PROW + PCOL
    )
    in_specs = (P(None, PROW, None, PCOL, None, None), P(None, PCOL, None, None), P(), P())
    out_specs = P(None, PCOL, None, None)
    return jax.shard_map(local, mesh=fine, in_specs=in_specs, out_specs=out_specs, check_vma=False)
```

```python
import jax
import jax.numpy as jnp
from jax import lax
from jax.sharding import PartitionSpec as P

LEVELS = 4
PROW = ("x", "core")
PCOL = ("y", "z")
RING = "z"


def node_order():
    ordering = []
    for depth_now in range(LEVELS - 1, -1, -1):
        ordering.extend(range(2**depth_now - 1, 2 ** (depth_now + 1) - 1))
    return ordering


def node_table(node_blocks, total_blocks):
    node_count = node_blocks.shape[0]
    ordered = jnp.array(node_order(), dtype=jnp.int32)
    node_ids = jnp.arange(node_count, dtype=jnp.int32)
    pick_sizes = (ordered[:, None] == node_ids[None, :]).astype(jnp.int32)
    level_sizes = jnp.sum(pick_sizes * node_blocks[None, :], axis=1)
    block_ends = jnp.cumsum(level_sizes)
    block_ids = jnp.arange(total_blocks, dtype=jnp.int32)
    positions = jnp.sum((block_ids[:, None] >= block_ends[None, :]).astype(jnp.int32), axis=1)
    return jnp.sum(
        (positions[:, None] == node_ids[None, :]).astype(jnp.int32) * ordered[None, :], axis=1
    )


def lookup(values_table, indices):
    positions_all = jnp.arange(values_table.shape[0], dtype=jnp.int32)
    return jnp.sum(
        (indices[:, None] == positions_all[None, :]).astype(jnp.int32) * values_table[None, :],
        axis=1,
    )


def panel_products(tile_stack, live_bits, vector):
    products = jnp.einsum("nxy,yw->nxw", tile_stack, vector, preferred_element_type=jnp.float32)
    return products * live_bits.astype(jnp.float32)[:, None, None]


def local(factor, right_side, node_blocks, front_mask):
    rows_local = factor.shape[0]
    cols_local = factor.shape[2]
    block_size = factor.shape[4]
    prow_count = lax.axis_size(PROW)
    pcol_count = lax.axis_size(PCOL)
    prow_index = lax.axis_index(PROW)
    pcol_index = lax.axis_index(PCOL)
    ring = lax.axis_size(RING)
    chunk_rows = block_size // ring
    total_blocks = rows_local * prow_count
    level_rows = pcol_count // prow_count
    piece_rows = block_size // pcol_count
    tile_grid = factor.reshape(rows_local, cols_local, block_size, block_size)
    tile_rows = factor.reshape(rows_local, cols_local * block_size, block_size)

    def column_tiles(first, col):
        return tile_rows[first:, col * block_size:(col + 1) * block_size]
    columns_in = right_side.reshape(cols_local, block_size, right_side.shape[3])
    block_node = node_table(node_blocks, total_blocks)
    row_ids = jnp.arange(rows_local, dtype=jnp.int32) * prow_count + prow_index
    col_ids = jnp.arange(cols_local, dtype=jnp.int32) * pcol_count + pcol_index
    row_nodes = lookup(block_node, row_ids)
    col_nodes = lookup(block_node, col_ids)
    node_ids = jnp.arange(node_blocks.shape[0], dtype=jnp.int32)
    pick_node = (col_nodes[:, None] == node_ids[None, :]).astype(jnp.int32)
    front_rows = jnp.sum(pick_node[:, :, None] * front_mask[None, :, :], axis=1)
    block_all = jnp.arange(total_blocks, dtype=jnp.int32)
    pick_row = (row_ids[:, None] == block_all[None, :]).astype(jnp.int32)
    front_bits = jnp.sum(pick_row[:, None, :] * front_rows[None, :, :], axis=2)
    diag_bits = (
        (row_nodes[:, None] == col_nodes[None, :]) & (row_ids[:, None] >= col_ids[None, :])
    ).astype(jnp.int32)

    def reduce_route(level_terms):
        rhs_width = level_terms.shape[2]
        pieces = level_terms.astype(jnp.bfloat16).reshape(pcol_count, chunk_rows, rhs_width)
        got = lax.all_to_all(pieces, PCOL, 0, 0, tiled=True)
        summed = jnp.sum(got.astype(jnp.float32), axis=0).astype(jnp.bfloat16)
        spread = jnp.broadcast_to(summed[None], (prow_count,) + summed.shape)
        gathered = lax.all_to_all(spread, PROW, 0, 0, tiled=True)
        arrived = lax.all_to_all(gathered, RING, 0, 0, tiled=True)
        return arrived.reshape(block_size, rhs_width)

    rhs_width = columns_in.shape[2]
    row_in_group = prow_index + prow_count * jnp.arange(level_rows, dtype=jnp.int32)
    owns_row = (row_in_group == pcol_index).astype(jnp.float32)
    partial_value = jnp.zeros((rows_local, block_size, rhs_width), jnp.float32)
    solved_list = []
    for section_now in range(LEVELS):
        first_row = section_now * level_rows
        after_row = first_row + level_rows
        if section_now == 0:
            rhs_column = columns_in[0]
        else:
            own_b = columns_in[section_now].astype(jnp.float32)
            contrib = owns_row[:, None, None] * own_b[None] - partial_value[first_row:after_row]
            rhs_column = reduce_route(contrib)
        diag_terms = panel_products(
            column_tiles(first_row, section_now)[:level_rows],
            diag_bits[first_row:after_row, section_now],
            rhs_column,
        )
        solved = reduce_route(diag_terms)
        solved_list.append(solved)
        if section_now + 1 < LEVELS:
            update_terms = panel_products(
                column_tiles(after_row, section_now), front_bits[after_row:, section_now], solved
            )
            partial_value = partial_value.at[after_row:].add(update_terms)
    solution = jnp.stack(solved_list)
    return solution.reshape(cols_local, 1, block_size, columns_in.shape[2])


def solution(mesh):
    fine = jax.sharding.Mesh(
        mesh.devices.reshape(4, mesh.devices.shape[0] // 4, 4, mesh.devices.shape[1] // 4), PROW + PCOL
    )
    in_specs = (P(None, PROW, None, PCOL, None, None), P(None, PCOL, None, None), P(), P())
    out_specs = P(None, PCOL, None, None)
    return jax.shard_map(local, mesh=fine, in_specs=in_specs, out_specs=out_specs, check_vma=False)
```

```python
import jax
import jax.numpy as jnp
from jax import lax
from jax.sharding import PartitionSpec as P

LEVELS = 4
PROW = ("x", "core")
PCOL = ("y", "z")
RING = "z"


def node_order():
    ordering = []
    for depth_now in range(LEVELS - 1, -1, -1):
        ordering.extend(range(2**depth_now - 1, 2 ** (depth_now + 1) - 1))
    return ordering


def node_table(node_blocks, total_blocks):
    node_count = node_blocks.shape[0]
    ordered = jnp.array(node_order(), dtype=jnp.int32)
    node_ids = jnp.arange(node_count, dtype=jnp.int32)
    pick_sizes = (ordered[:, None] == node_ids[None, :]).astype(jnp.int32)
    level_sizes = jnp.sum(pick_sizes * node_blocks[None, :], axis=1)
    block_ends = jnp.cumsum(level_sizes)
    block_ids = jnp.arange(total_blocks, dtype=jnp.int32)
    positions = jnp.sum((block_ids[:, None] >= block_ends[None, :]).astype(jnp.int32), axis=1)
    return jnp.sum(
        (positions[:, None] == node_ids[None, :]).astype(jnp.int32) * ordered[None, :], axis=1
    )


def lookup(values_table, indices):
    positions_all = jnp.arange(values_table.shape[0], dtype=jnp.int32)
    return jnp.sum(
        (indices[:, None] == positions_all[None, :]).astype(jnp.int32) * values_table[None, :],
        axis=1,
    )


def panel_products(tile_stack, live_bits, vector):
    products = jnp.einsum("nxy,yw->nxw", tile_stack, vector, preferred_element_type=jnp.float32)
    return products * live_bits.astype(jnp.float32)[:, None, None]


def local(factor, right_side, node_blocks, front_mask):
    rows_local = factor.shape[0]
    cols_local = factor.shape[2]
    block_size = factor.shape[4]
    prow_count = lax.axis_size(PROW)
    pcol_count = lax.axis_size(PCOL)
    prow_index = lax.axis_index(PROW)
    pcol_index = lax.axis_index(PCOL)
    ring = lax.axis_size(RING)
    chunk_rows = block_size // ring
    total_blocks = rows_local * prow_count
    level_rows = pcol_count // prow_count
    piece_rows = block_size // pcol_count
    tile_grid = factor.reshape(rows_local, cols_local, block_size, block_size)
    tile_rows = factor.reshape(rows_local, cols_local * block_size, block_size)

    def column_tiles(first, col):
        return tile_rows[first:, col * block_size:(col + 1) * block_size]
    columns_in = right_side.reshape(cols_local, block_size, right_side.shape[3])
    rhs_width = columns_in.shape[2]
    block_node = node_table(node_blocks, total_blocks)
    row_ids = jnp.arange(rows_local, dtype=jnp.int32) * prow_count + prow_index
    col_ids = jnp.arange(cols_local, dtype=jnp.int32) * pcol_count + pcol_index
    row_nodes = lookup(block_node, row_ids)
    col_nodes = lookup(block_node, col_ids)
    node_ids = jnp.arange(node_blocks.shape[0], dtype=jnp.int32)
    pick_node = (col_nodes[:, None] == node_ids[None, :]).astype(jnp.int32)
    front_rows = jnp.sum(pick_node[:, :, None] * front_mask[None, :, :], axis=1)
    block_all = jnp.arange(total_blocks, dtype=jnp.int32)
    pick_row = (row_ids[:, None] == block_all[None, :]).astype(jnp.int32)
    front_bits = jnp.sum(pick_row[:, None, :] * front_rows[None, :, :], axis=2)
    diag_bits = (
        (row_nodes[:, None] == col_nodes[None, :]) & (row_ids[:, None] >= col_ids[None, :])
    ).astype(jnp.int32)

    def reduce_gather(level_terms):
        pieces = level_terms.astype(jnp.bfloat16).reshape(pcol_count, chunk_rows, rhs_width)
        got = lax.all_to_all(pieces, PCOL, 0, 0, tiled=True)
        summed = jnp.sum(got.astype(jnp.float32), axis=0).astype(jnp.bfloat16)
        spread = jnp.broadcast_to(summed[None], (prow_count,) + summed.shape)
        return lax.all_to_all(spread, PROW, 0, 0, tiled=True)

    def route_ring(gathered, extra):
        flat = gathered.reshape(ring, chunk_rows * rhs_width)
        if extra is not None:
            flat = jnp.concatenate([flat, extra], axis=1)
        arrived = lax.all_to_all(flat, RING, 0, 0, tiled=True)
        solved = arrived[:, : chunk_rows * rhs_width].reshape(block_size, rhs_width)
        return solved, (arrived[:, chunk_rows * rhs_width :] if extra is not None else None)

    def ring_chunks(section):
        tiles = column_tiles(section * level_rows, section)[:level_rows]
        split = tiles.reshape(level_rows, block_size, ring, chunk_rows)
        return jnp.transpose(split, (2, 0, 1, 3)).reshape(ring, level_rows * block_size * chunk_rows)

    ring_index = pcol_index % ring
    group_base = pcol_index - ring_index
    row_in_group = prow_index + prow_count * jnp.arange(level_rows, dtype=jnp.int32)
    owns_row = (row_in_group == pcol_index).astype(jnp.float32)
    ring_cols = group_base + jnp.arange(ring, dtype=jnp.int32)

    partial_value = jnp.zeros((rows_local, block_size, rhs_width), jnp.float32)
    solved_list = []
    chunks_in = None
    for section_now in range(LEVELS):
        first_row = section_now * level_rows
        after_row = first_row + level_rows
        if section_now == 0:
            diag_terms = panel_products(
                column_tiles(first_row, section_now)[:level_rows],
                diag_bits[first_row:after_row, section_now],
                columns_in[0],
            )
        else:
            own_b = columns_in[section_now].astype(jnp.float32)
            contrib = owns_row[:, None, None] * own_b[None] - partial_value[first_row:after_row]
            rhs_chunks = reduce_gather(contrib)
            level_row_ids = section_now * pcol_count + row_in_group
            level_col_ids = section_now * pcol_count + ring_cols
            row_node = lookup(block_node, level_row_ids)
            col_node = lookup(block_node, level_col_ids)
            live = (col_node[:, None] == row_node[None, :]) & (level_col_ids[:, None] <= level_row_ids[None, :])
            tiles = chunks_in.reshape(ring, level_rows, block_size, chunk_rows)
            tiles = tiles * live.astype(jnp.bfloat16)[:, :, None, None]
            tiles = jnp.transpose(tiles, (1, 2, 0, 3)).reshape(level_rows, block_size, block_size)
            diag_terms = jnp.einsum(
                "kxy,yw->kxw", tiles, rhs_chunks.reshape(block_size, rhs_width), preferred_element_type=jnp.float32
            )
        extra = ring_chunks(section_now + 1) if section_now + 1 < LEVELS else None
        solved, chunks_in = route_ring(reduce_gather(diag_terms), extra)
        solved_list.append(solved)
        if section_now + 1 < LEVELS:
            update_terms = panel_products(
                column_tiles(after_row, section_now), front_bits[after_row:, section_now], solved
            )
            partial_value = partial_value.at[after_row:].add(update_terms)
    solution = jnp.stack(solved_list)
    return solution.reshape(cols_local, 1, block_size, columns_in.shape[2])


def solution(mesh):
    fine = jax.sharding.Mesh(
        mesh.devices.reshape(4, mesh.devices.shape[0] // 4, 4, mesh.devices.shape[1] // 4), PROW + PCOL
    )
    in_specs = (P(None, PROW, None, PCOL, None, None), P(None, PCOL, None, None), P(), P())
    out_specs = P(None, PCOL, None, None)
    return jax.shard_map(local, mesh=fine, in_specs=in_specs, out_specs=out_specs, check_vma=False)
```

```python
import jax
import jax.numpy as jnp
from jax import lax
from jax.sharding import PartitionSpec as P

LEVELS = 4
PROW = ("x", "core")
PCOL = ("y", "z")
RING = "z"


def node_order():
    ordering = []
    for depth_now in range(LEVELS - 1, -1, -1):
        ordering.extend(range(2**depth_now - 1, 2 ** (depth_now + 1) - 1))
    return ordering


def node_table(node_blocks, total_blocks):
    node_count = node_blocks.shape[0]
    ordered = jnp.array(node_order(), dtype=jnp.int32)
    node_ids = jnp.arange(node_count, dtype=jnp.int32)
    pick_sizes = (ordered[:, None] == node_ids[None, :]).astype(jnp.int32)
    level_sizes = jnp.sum(pick_sizes * node_blocks[None, :], axis=1)
    block_ends = jnp.cumsum(level_sizes)
    block_ids = jnp.arange(total_blocks, dtype=jnp.int32)
    positions = jnp.sum((block_ids[:, None] >= block_ends[None, :]).astype(jnp.int32), axis=1)
    return jnp.sum(
        (positions[:, None] == node_ids[None, :]).astype(jnp.int32) * ordered[None, :], axis=1
    )


def lookup(values_table, indices):
    positions_all = jnp.arange(values_table.shape[0], dtype=jnp.int32)
    return jnp.sum(
        (indices[:, None] == positions_all[None, :]).astype(jnp.int32) * values_table[None, :],
        axis=1,
    )


def panel_products(tile_stack, live_bits, vector):
    products = jnp.einsum("nxy,yw->nxw", tile_stack, vector, preferred_element_type=jnp.float32)
    return products * live_bits.astype(jnp.float32)[:, None, None]


def local(factor, right_side, node_blocks, front_mask):
    rows_local = factor.shape[0]
    cols_local = factor.shape[2]
    block_size = factor.shape[4]
    prow_count = lax.axis_size(PROW)
    pcol_count = lax.axis_size(PCOL)
    prow_index = lax.axis_index(PROW)
    pcol_index = lax.axis_index(PCOL)
    ring = lax.axis_size(RING)
    chunk_rows = block_size // ring
    total_blocks = rows_local * prow_count
    level_rows = pcol_count // prow_count
    piece_rows = block_size // pcol_count
    tile_grid = factor.reshape(rows_local, cols_local, block_size, block_size)
    tile_rows = factor.reshape(rows_local, cols_local * block_size, block_size)

    def column_tiles(first, col):
        return tile_rows[first:, col * block_size:(col + 1) * block_size]
    columns_in = right_side.reshape(cols_local, block_size, right_side.shape[3])
    block_node = node_table(node_blocks, total_blocks)
    row_ids = jnp.arange(rows_local, dtype=jnp.int32) * prow_count + prow_index
    col_ids = jnp.arange(cols_local, dtype=jnp.int32) * pcol_count + pcol_index
    row_nodes = lookup(block_node, row_ids)
    col_nodes = lookup(block_node, col_ids)
    node_ids = jnp.arange(node_blocks.shape[0], dtype=jnp.int32)
    pick_node = (col_nodes[:, None] == node_ids[None, :]).astype(jnp.int32)
    front_rows = jnp.sum(pick_node[:, :, None] * front_mask[None, :, :], axis=1)
    block_all = jnp.arange(total_blocks, dtype=jnp.int32)
    pick_row = (row_ids[:, None] == block_all[None, :]).astype(jnp.int32)
    front_bits = jnp.sum(pick_row[:, None, :] * front_rows[None, :, :], axis=2)
    diag_bits = (
        (row_nodes[:, None] == col_nodes[None, :]) & (row_ids[:, None] >= col_ids[None, :])
    ).astype(jnp.int32)

    def reduce_route(level_terms):
        rhs_width = level_terms.shape[2]
        pieces = level_terms.astype(jnp.bfloat16).reshape(pcol_count, chunk_rows, rhs_width)
        got = lax.all_to_all(pieces, PCOL, 0, 0, tiled=True)
        summed = jnp.sum(got.astype(jnp.float32), axis=0).astype(jnp.bfloat16)
        spread = jnp.broadcast_to(summed[None], (prow_count,) + summed.shape)
        gathered = lax.all_to_all(spread, PROW, 0, 0, tiled=True)
        arrived = lax.all_to_all(gathered, RING, 0, 0, tiled=True)
        return arrived.reshape(block_size, rhs_width)

    rhs_width = columns_in.shape[2]
    partial_levels = [None] * LEVELS
    solved_list = []
    for section_now in range(LEVELS):
        first_row = section_now * level_rows
        after_row = first_row + level_rows
        if section_now == 0:
            rhs_column = columns_in[0]
        else:
            update = reduce_route(partial_levels[section_now]).astype(jnp.float32)
            rhs_column = (columns_in[section_now].astype(jnp.float32) - update).astype(jnp.bfloat16)
        diag_terms = panel_products(
            column_tiles(first_row, section_now)[:level_rows],
            diag_bits[first_row:after_row, section_now],
            rhs_column,
        )
        solved = reduce_route(diag_terms)
        solved_list.append(solved)
        for later in range(section_now + 1, LEVELS):
            later_row = later * level_rows
            update_terms = panel_products(
                column_tiles(later_row, section_now)[:level_rows],
                front_bits[later_row:later_row + level_rows, section_now],
                solved,
            )
            if partial_levels[later] is None:
                partial_levels[later] = update_terms
            else:
                partial_levels[later] = partial_levels[later] + update_terms
    solution = jnp.stack(solved_list)
    return solution.reshape(cols_local, 1, block_size, columns_in.shape[2])


def solution(mesh):
    fine = jax.sharding.Mesh(
        mesh.devices.reshape(4, mesh.devices.shape[0] // 4, 4, mesh.devices.shape[1] // 4), PROW + PCOL
    )
    in_specs = (P(None, PROW, None, PCOL, None, None), P(None, PCOL, None, None), P(), P())
    out_specs = P(None, PCOL, None, None)
    return jax.shard_map(local, mesh=fine, in_specs=in_specs, out_specs=out_specs, check_vma=False)
```

```python
import jax
import jax.numpy as jnp
from jax import lax
from jax.sharding import PartitionSpec as P

LEVELS = 4
PROW = ("x", "core")
PCOL = ("y", "z")
RING = "z"


def node_order():
    ordering = []
    for depth_now in range(LEVELS - 1, -1, -1):
        ordering.extend(range(2**depth_now - 1, 2 ** (depth_now + 1) - 1))
    return ordering


def node_table(node_blocks, total_blocks):
    node_count = node_blocks.shape[0]
    ordered = jnp.array(node_order(), dtype=jnp.int32)
    node_ids = jnp.arange(node_count, dtype=jnp.int32)
    pick_sizes = (ordered[:, None] == node_ids[None, :]).astype(jnp.int32)
    level_sizes = jnp.sum(pick_sizes * node_blocks[None, :], axis=1)
    block_ends = jnp.cumsum(level_sizes)
    block_ids = jnp.arange(total_blocks, dtype=jnp.int32)
    positions = jnp.sum((block_ids[:, None] >= block_ends[None, :]).astype(jnp.int32), axis=1)
    return jnp.sum(
        (positions[:, None] == node_ids[None, :]).astype(jnp.int32) * ordered[None, :], axis=1
    )


def lookup(values_table, indices):
    positions_all = jnp.arange(values_table.shape[0], dtype=jnp.int32)
    return jnp.sum(
        (indices[:, None] == positions_all[None, :]).astype(jnp.int32) * values_table[None, :],
        axis=1,
    )


def panel_products(tile_stack, live_bits, vector):
    products = jnp.einsum("nxy,yw->nxw", tile_stack, vector, preferred_element_type=jnp.float32)
    return products * live_bits.astype(jnp.float32)[:, None, None]


def local(factor, right_side, node_blocks, front_mask):
    rows_local = factor.shape[0]
    cols_local = factor.shape[2]
    block_size = factor.shape[4]
    prow_count = lax.axis_size(PROW)
    pcol_count = lax.axis_size(PCOL)
    prow_index = lax.axis_index(PROW)
    pcol_index = lax.axis_index(PCOL)
    ring = lax.axis_size(RING)
    chunk_rows = block_size // ring
    total_blocks = rows_local * prow_count
    level_rows = pcol_count // prow_count
    piece_rows = block_size // pcol_count
    tile_grid = factor.reshape(rows_local, cols_local, block_size, block_size)
    tile_rows = factor.reshape(rows_local, cols_local * block_size, block_size)

    def column_tiles(first, col):
        return tile_rows[first:, col * block_size:(col + 1) * block_size]
    columns_in = right_side.reshape(cols_local, block_size, right_side.shape[3])
    block_node = node_table(node_blocks, total_blocks)
    row_ids = jnp.arange(rows_local, dtype=jnp.int32) * prow_count + prow_index
    col_ids = jnp.arange(cols_local, dtype=jnp.int32) * pcol_count + pcol_index
    col_nodes = lookup(block_node, col_ids)
    node_ids = jnp.arange(node_blocks.shape[0], dtype=jnp.int32)
    pick_node = (col_nodes[:, None] == node_ids[None, :]).astype(jnp.int32)
    front_rows = jnp.sum(pick_node[:, :, None] * front_mask[None, :, :], axis=1)
    block_all = jnp.arange(total_blocks, dtype=jnp.int32)
    pick_row = (row_ids[:, None] == block_all[None, :]).astype(jnp.int32)
    front_bits = jnp.sum(pick_row[:, None, :] * front_rows[None, :, :], axis=2)
    ordered_ids = jnp.array(node_order(), dtype=jnp.int32)
    pick_sizes = (ordered_ids[:, None] == node_ids[None, :]).astype(jnp.int32)
    block_ends = jnp.cumsum(jnp.sum(pick_sizes * node_blocks[None, :], axis=1))
    row_pos = jnp.sum((row_ids[:, None] >= block_ends[None, :]).astype(jnp.int32), axis=1)
    col_pos = jnp.sum((col_ids[:, None] >= block_ends[None, :]).astype(jnp.int32), axis=1)
    diag_bits = ((row_pos[:, None] == col_pos[None, :]) & (row_ids[:, None] >= col_ids[None, :])).astype(
        jnp.int32
    )

    def reduce_route(level_terms):
        rhs_width = level_terms.shape[2]
        pieces = level_terms.astype(jnp.bfloat16).reshape(pcol_count, chunk_rows, rhs_width)
        got = lax.all_to_all(pieces, PCOL, 0, 0, tiled=True)
        summed = jnp.sum(got.astype(jnp.float32), axis=0).astype(jnp.bfloat16)
        spread = jnp.broadcast_to(summed[None], (prow_count,) + summed.shape)
        gathered = lax.all_to_all(spread, PROW, 0, 0, tiled=True)
        arrived = lax.all_to_all(gathered, RING, 0, 0, tiled=True)
        return arrived.reshape(block_size, rhs_width)

    rhs_width = columns_in.shape[2]
    partial_levels = [None] * LEVELS
    solution = jnp.zeros((LEVELS, block_size, rhs_width), columns_in.dtype)
    for section_now in range(LEVELS):
        first_row = section_now * level_rows
        after_row = first_row + level_rows
        if section_now == 0:
            rhs_column = columns_in[0]
        else:
            update = reduce_route(partial_levels[section_now]).astype(jnp.float32)
            rhs_column = (columns_in[section_now].astype(jnp.float32) - update).astype(jnp.bfloat16)
        diag_terms = panel_products(
            column_tiles(first_row, section_now)[:level_rows],
            diag_bits[first_row:after_row, section_now],
            rhs_column,
        )
        solved = reduce_route(diag_terms)
        solution = solution.at[section_now].set(solved)
        for later in range(section_now + 1, LEVELS):
            later_row = later * level_rows
            update_terms = panel_products(
                column_tiles(later_row, section_now)[:level_rows],
                front_bits[later_row:later_row + level_rows, section_now],
                solved,
            )
            if partial_levels[later] is None:
                partial_levels[later] = update_terms
            else:
                partial_levels[later] = partial_levels[later] + update_terms
    return solution.reshape(cols_local, 1, block_size, columns_in.shape[2])


def solution(mesh):
    fine = jax.sharding.Mesh(
        mesh.devices.reshape(4, mesh.devices.shape[0] // 4, 4, mesh.devices.shape[1] // 4), PROW + PCOL
    )
    in_specs = (P(None, PROW, None, PCOL, None, None), P(None, PCOL, None, None), P(), P())
    out_specs = P(None, PCOL, None, None)
    return jax.shard_map(local, mesh=fine, in_specs=in_specs, out_specs=out_specs, check_vma=False)
```

```python
import jax
import jax.numpy as jnp
from jax import lax
from jax.sharding import PartitionSpec as P

LEVELS = 4
PROW = ("x", "core")
PCOL = ("y", "z")
RING = "z"


def node_order():
    ordering = []
    for depth_now in range(LEVELS - 1, -1, -1):
        ordering.extend(range(2**depth_now - 1, 2 ** (depth_now + 1) - 1))
    return ordering


def node_table(node_blocks, total_blocks):
    node_count = node_blocks.shape[0]
    ordered = jnp.array(node_order(), dtype=jnp.int32)
    node_ids = jnp.arange(node_count, dtype=jnp.int32)
    pick_sizes = (ordered[:, None] == node_ids[None, :]).astype(jnp.int32)
    level_sizes = jnp.sum(pick_sizes * node_blocks[None, :], axis=1)
    block_ends = jnp.cumsum(level_sizes)
    block_ids = jnp.arange(total_blocks, dtype=jnp.int32)
    positions = jnp.sum((block_ids[:, None] >= block_ends[None, :]).astype(jnp.int32), axis=1)
    return jnp.sum(
        (positions[:, None] == node_ids[None, :]).astype(jnp.int32) * ordered[None, :], axis=1
    )


def lookup(values_table, indices):
    positions_all = jnp.arange(values_table.shape[0], dtype=jnp.int32)
    return jnp.sum(
        (indices[:, None] == positions_all[None, :]).astype(jnp.int32) * values_table[None, :],
        axis=1,
    )


def panel_products(tile_stack, live_bits, vector):
    products = jnp.einsum("nxy,yw->nxw", tile_stack, vector, preferred_element_type=jnp.float32)
    return products * live_bits.astype(jnp.float32)[:, None, None]


def local(factor, right_side, node_blocks, front_mask):
    rows_local = factor.shape[0]
    cols_local = factor.shape[2]
    block_size = factor.shape[4]
    prow_count = lax.axis_size(PROW)
    pcol_count = lax.axis_size(PCOL)
    prow_index = lax.axis_index(PROW)
    pcol_index = lax.axis_index(PCOL)
    ring = lax.axis_size(RING)
    chunk_rows = block_size // ring
    total_blocks = rows_local * prow_count
    level_rows = pcol_count // prow_count
    piece_rows = block_size // pcol_count
    tile_grid = factor.reshape(rows_local, cols_local, block_size, block_size)
    tile_rows = factor.reshape(rows_local, cols_local * block_size, block_size)

    def column_tiles(first, col):
        return tile_rows[first:, col * block_size:(col + 1) * block_size]
    columns_in = right_side.reshape(cols_local, block_size, right_side.shape[3])
    block_node = node_table(node_blocks, total_blocks)
    row_ids = jnp.arange(rows_local, dtype=jnp.int32) * prow_count + prow_index
    col_ids = jnp.arange(cols_local, dtype=jnp.int32) * pcol_count + pcol_index
    row_nodes = lookup(block_node, row_ids)
    col_nodes = lookup(block_node, col_ids)
    node_ids = jnp.arange(node_blocks.shape[0], dtype=jnp.int32)
    pick_node = (col_nodes[:, None] == node_ids[None, :]).astype(jnp.int32)
    front_rows = jnp.sum(pick_node[:, :, None] * front_mask[None, :, :], axis=1)
    block_all = jnp.arange(total_blocks, dtype=jnp.int32)
    pick_row = (row_ids[:, None] == block_all[None, :]).astype(jnp.int32)
    front_bits = jnp.sum(pick_row[:, None, :] * front_rows[None, :, :], axis=2)
    diag_bits = (
        (row_nodes[:, None] == col_nodes[None, :]) & (row_ids[:, None] >= col_ids[None, :])
    ).astype(jnp.int32)

    def reduce_route(level_terms):
        rhs_width = level_terms.shape[2]
        pieces = level_terms.astype(jnp.bfloat16).reshape(level_rows, ring, chunk_rows, rhs_width)
        pieces = jnp.transpose(pieces, (1, 0, 2, 3)).reshape(pcol_count, chunk_rows, rhs_width)
        got = lax.all_to_all(pieces, PCOL[::-1], 0, 0, tiled=True)
        summed = jnp.sum(got.astype(jnp.float32), axis=0).astype(jnp.bfloat16)
        spread = jnp.broadcast_to(summed[None], (prow_count,) + summed.shape)
        gathered = lax.all_to_all(spread, PROW, 0, 0, tiled=True)
        arrived = lax.all_to_all(gathered, RING, 0, 0, tiled=True)
        return arrived.reshape(block_size, rhs_width)

    rhs_width = columns_in.shape[2]
    partial_levels = [None] * LEVELS
    solved_list = []
    for section_now in range(LEVELS):
        first_row = section_now * level_rows
        after_row = first_row + level_rows
        if section_now == 0:
            rhs_column = columns_in[0]
        else:
            update = reduce_route(partial_levels[section_now]).astype(jnp.float32)
            rhs_column = (columns_in[section_now].astype(jnp.float32) - update).astype(jnp.bfloat16)
        diag_terms = panel_products(
            column_tiles(first_row, section_now)[:level_rows],
            diag_bits[first_row:after_row, section_now],
            rhs_column,
        )
        solved = reduce_route(diag_terms)
        solved_list.append(solved)
        for later in range(section_now + 1, LEVELS):
            later_row = later * level_rows
            update_terms = panel_products(
                column_tiles(later_row, section_now)[:level_rows],
                front_bits[later_row:later_row + level_rows, section_now],
                solved,
            )
            if partial_levels[later] is None:
                partial_levels[later] = update_terms
            else:
                partial_levels[later] = partial_levels[later] + update_terms
    solution = jnp.stack(solved_list)
    return solution.reshape(cols_local, 1, block_size, columns_in.shape[2])


def solution(mesh):
    fine = jax.sharding.Mesh(
        mesh.devices.reshape(4, mesh.devices.shape[0] // 4, 4, mesh.devices.shape[1] // 4), PROW + PCOL
    )
    in_specs = (P(None, PROW, None, PCOL, None, None), P(None, PCOL, None, None), P(), P())
    out_specs = P(None, PCOL, None, None)
    return jax.shard_map(local, mesh=fine, in_specs=in_specs, out_specs=out_specs, check_vma=False)
```

```python
import jax
import jax.numpy as jnp
from jax import lax
from jax.sharding import PartitionSpec as P

LEVELS = 4
PROW = ("x", "core")
PCOL = ("y", "z")
RING = "z"


def node_order():
    ordering = []
    for depth_now in range(LEVELS - 1, -1, -1):
        ordering.extend(range(2**depth_now - 1, 2 ** (depth_now + 1) - 1))
    return ordering


def node_table(node_blocks, total_blocks):
    node_count = node_blocks.shape[0]
    ordered = jnp.array(node_order(), dtype=jnp.int32)
    node_ids = jnp.arange(node_count, dtype=jnp.int32)
    pick_sizes = (ordered[:, None] == node_ids[None, :]).astype(jnp.int32)
    level_sizes = jnp.sum(pick_sizes * node_blocks[None, :], axis=1)
    block_ends = jnp.cumsum(level_sizes)
    block_ids = jnp.arange(total_blocks, dtype=jnp.int32)
    positions = jnp.sum((block_ids[:, None] >= block_ends[None, :]).astype(jnp.int32), axis=1)
    return jnp.sum(
        (positions[:, None] == node_ids[None, :]).astype(jnp.int32) * ordered[None, :], axis=1
    )


def lookup(values_table, indices):
    positions_all = jnp.arange(values_table.shape[0], dtype=jnp.int32)
    return jnp.sum(
        (indices[:, None] == positions_all[None, :]).astype(jnp.int32) * values_table[None, :],
        axis=1,
    )


def panel_products(tile_stack, live_bits, vector):
    products = jnp.einsum("nxy,yw->nxw", tile_stack, vector, preferred_element_type=jnp.float32)
    return products * live_bits.astype(jnp.float32)[:, None, None]


def local(factor, right_side, node_blocks, front_mask):
    rows_local = factor.shape[0]
    cols_local = factor.shape[2]
    block_size = factor.shape[4]
    prow_count = lax.axis_size(PROW)
    pcol_count = lax.axis_size(PCOL)
    prow_index = lax.axis_index(PROW)
    pcol_index = lax.axis_index(PCOL)
    ring = lax.axis_size(RING)
    chunk_rows = block_size // ring
    total_blocks = rows_local * prow_count
    level_rows = pcol_count // prow_count
    piece_rows = block_size // pcol_count
    tile_grid = factor.reshape(rows_local, cols_local, block_size, block_size)
    tile_rows = factor.reshape(rows_local, cols_local * block_size, block_size)

    def column_tiles(first, col):
        return tile_rows[first:, col * block_size:(col + 1) * block_size]
    columns_in = right_side.reshape(cols_local, block_size, right_side.shape[3])
    block_node = node_table(node_blocks, total_blocks)
    row_ids = jnp.arange(rows_local, dtype=jnp.int32) * prow_count + prow_index
    col_ids = jnp.arange(cols_local, dtype=jnp.int32) * pcol_count + pcol_index
    row_nodes = lookup(block_node, row_ids)
    col_nodes = lookup(block_node, col_ids)
    node_ids = jnp.arange(node_blocks.shape[0], dtype=jnp.int32)
    pick_node = (col_nodes[:, None] == node_ids[None, :]).astype(jnp.int32)
    front_rows = jnp.sum(pick_node[:, :, None] * front_mask[None, :, :], axis=1)
    block_all = jnp.arange(total_blocks, dtype=jnp.int32)
    pick_row = (row_ids[:, None] == block_all[None, :]).astype(jnp.int32)
    front_bits = jnp.sum(pick_row[:, None, :] * front_rows[None, :, :], axis=2)
    diag_bits = (
        (row_nodes[:, None] == col_nodes[None, :]) & (row_ids[:, None] >= col_ids[None, :])
    ).astype(jnp.int32)

    def reduce_route(level_terms):
        rhs_width = level_terms.shape[2]
        pieces = level_terms.astype(jnp.bfloat16).reshape(pcol_count, chunk_rows, rhs_width)
        got = lax.all_to_all(pieces, PCOL, 0, 0, tiled=True)
        summed = jnp.sum(got.astype(jnp.float32), axis=0).astype(jnp.bfloat16)
        spread = jnp.broadcast_to(summed[None], (prow_count,) + summed.shape)
        gathered = lax.all_to_all(spread, PROW[::-1], 0, 0, tiled=True)
        core_count = lax.axis_size(PROW[1])
        gathered = jnp.transpose(
            gathered.reshape((core_count, prow_count // core_count) + summed.shape), (1, 0, 2, 3)
        ).reshape((prow_count,) + summed.shape)
        arrived = lax.all_to_all(gathered, RING, 0, 0, tiled=True)
        return arrived.reshape(block_size, rhs_width)

    rhs_width = columns_in.shape[2]
    partial_levels = [None] * LEVELS
    solved_list = []
    for section_now in range(LEVELS):
        first_row = section_now * level_rows
        after_row = first_row + level_rows
        if section_now == 0:
            rhs_column = columns_in[0]
        else:
            update = reduce_route(partial_levels[section_now]).astype(jnp.float32)
            rhs_column = (columns_in[section_now].astype(jnp.float32) - update).astype(jnp.bfloat16)
        diag_terms = panel_products(
            column_tiles(first_row, section_now)[:level_rows],
            diag_bits[first_row:after_row, section_now],
            rhs_column,
        )
        solved = reduce_route(diag_terms)
        solved_list.append(solved)
        for later in range(section_now + 1, LEVELS):
            later_row = later * level_rows
            update_terms = panel_products(
                column_tiles(later_row, section_now)[:level_rows],
                front_bits[later_row:later_row + level_rows, section_now],
                solved,
            )
            if partial_levels[later] is None:
                partial_levels[later] = update_terms
            else:
                partial_levels[later] = partial_levels[later] + update_terms
    solution = jnp.stack(solved_list)
    return solution.reshape(cols_local, 1, block_size, columns_in.shape[2])


def solution(mesh):
    fine = jax.sharding.Mesh(
        mesh.devices.reshape(4, mesh.devices.shape[0] // 4, 4, mesh.devices.shape[1] // 4), PROW + PCOL
    )
    in_specs = (P(None, PROW, None, PCOL, None, None), P(None, PCOL, None, None), P(), P())
    out_specs = P(None, PCOL, None, None)
    return jax.shard_map(local, mesh=fine, in_specs=in_specs, out_specs=out_specs, check_vma=False)
```

```python
import jax
import jax.numpy as jnp
from jax import lax
from jax.sharding import PartitionSpec as P

LEVELS = 4
PROW = ("x", "core")
PCOL = ("y", "z")
RING = "z"


def node_order():
    ordering = []
    for depth_now in range(LEVELS - 1, -1, -1):
        ordering.extend(range(2**depth_now - 1, 2 ** (depth_now + 1) - 1))
    return ordering


def node_table(node_blocks, total_blocks):
    node_count = node_blocks.shape[0]
    ordered = jnp.array(node_order(), dtype=jnp.int32)
    node_ids = jnp.arange(node_count, dtype=jnp.int32)
    pick_sizes = (ordered[:, None] == node_ids[None, :]).astype(jnp.int32)
    level_sizes = jnp.sum(pick_sizes * node_blocks[None, :], axis=1)
    block_ends = jnp.cumsum(level_sizes)
    block_ids = jnp.arange(total_blocks, dtype=jnp.int32)
    positions = jnp.sum((block_ids[:, None] >= block_ends[None, :]).astype(jnp.int32), axis=1)
    return jnp.sum(
        (positions[:, None] == node_ids[None, :]).astype(jnp.int32) * ordered[None, :], axis=1
    )


def lookup(values_table, indices):
    positions_all = jnp.arange(values_table.shape[0], dtype=jnp.int32)
    return jnp.sum(
        (indices[:, None] == positions_all[None, :]).astype(jnp.int32) * values_table[None, :],
        axis=1,
    )


def panel_products(tile_stack, live_bits, vector):
    products = jnp.einsum("nxy,yw->nxw", tile_stack, vector, preferred_element_type=jnp.float32)
    return products * live_bits.astype(jnp.float32)[:, None, None]


def local(factor, right_side, node_blocks, front_mask):
    rows_local = factor.shape[0]
    cols_local = factor.shape[2]
    block_size = factor.shape[4]
    prow_count = lax.axis_size(PROW)
    pcol_count = lax.axis_size(PCOL)
    prow_index = lax.axis_index(PROW)
    pcol_index = lax.axis_index(PCOL)
    ring = lax.axis_size(RING)
    chunk_rows = block_size // ring
    total_blocks = rows_local * prow_count
    level_rows = pcol_count // prow_count
    piece_rows = block_size // pcol_count
    tile_grid = factor.reshape(rows_local, cols_local, block_size, block_size)
    tile_rows = factor.reshape(rows_local, cols_local * block_size, block_size)

    def column_tiles(first, col):
        return tile_rows[first:, col * block_size:(col + 1) * block_size]
    columns_in = right_side.reshape(cols_local, block_size, right_side.shape[3])
    block_node = node_table(node_blocks, total_blocks)
    row_ids = jnp.arange(rows_local, dtype=jnp.int32) * prow_count + prow_index
    col_ids = jnp.arange(cols_local, dtype=jnp.int32) * pcol_count + pcol_index
    col_nodes = lookup(block_node, col_ids)
    node_ids = jnp.arange(node_blocks.shape[0], dtype=jnp.int32)
    pick_node = (col_nodes[:, None] == node_ids[None, :]).astype(jnp.int32)
    front_rows = jnp.sum(pick_node[:, :, None] * front_mask[None, :, :], axis=1)
    block_all = jnp.arange(total_blocks, dtype=jnp.int32)
    pick_row = (row_ids[:, None] == block_all[None, :]).astype(jnp.int32)
    front_bits = jnp.sum(pick_row[:, None, :] * front_rows[None, :, :], axis=2)
    ordered_ids = jnp.array(node_order(), dtype=jnp.int32)
    pick_sizes = (ordered_ids[:, None] == node_ids[None, :]).astype(jnp.int32)
    block_ends = jnp.cumsum(jnp.sum(pick_sizes * node_blocks[None, :], axis=1))
    row_pos = jnp.sum((row_ids[:, None] >= block_ends[None, :]).astype(jnp.int32), axis=1)
    col_pos = jnp.sum((col_ids[:, None] >= block_ends[None, :]).astype(jnp.int32), axis=1)
    diag_bits = ((row_pos[:, None] == col_pos[None, :]) & (row_ids[:, None] >= col_ids[None, :])).astype(
        jnp.int32
    )

    def reduce_route(level_terms):
        rhs_width = level_terms.shape[2]
        pieces = level_terms.astype(jnp.bfloat16).reshape(pcol_count, chunk_rows, rhs_width)
        got = lax.all_to_all(pieces, PCOL, 0, 0, tiled=True)
        summed = jnp.sum(got.astype(jnp.float32), axis=0).astype(jnp.bfloat16)
        spread = jnp.broadcast_to(summed[None], (prow_count,) + summed.shape)
        gathered = lax.all_to_all(spread, PROW, 0, 0, tiled=True)
        arrived = lax.all_to_all(gathered, RING, 0, 0, tiled=True)
        return arrived.reshape(block_size, rhs_width)

    rhs_width = columns_in.shape[2]
    row_in_group = prow_index + prow_count * jnp.arange(level_rows, dtype=jnp.int32)
    owns_row = (row_in_group == pcol_index).astype(jnp.float32)
    partial_levels = [None] * LEVELS
    solution = jnp.zeros((LEVELS, block_size, rhs_width), columns_in.dtype)
    for section_now in range(LEVELS):
        first_row = section_now * level_rows
        after_row = first_row + level_rows
        if section_now == 0:
            rhs_column = columns_in[0]
        else:
            own_b = columns_in[section_now].astype(jnp.float32)
            rhs_column = reduce_route(owns_row[:, None, None] * own_b[None] - partial_levels[section_now])
        diag_terms = panel_products(
            column_tiles(first_row, section_now)[:level_rows],
            diag_bits[first_row:after_row, section_now],
            rhs_column,
        )
        solved = reduce_route(diag_terms)
        solution = solution.at[section_now].set(solved)
        for later in range(section_now + 1, LEVELS):
            later_row = later * level_rows
            update_terms = panel_products(
                column_tiles(later_row, section_now)[:level_rows],
                front_bits[later_row:later_row + level_rows, section_now],
                solved,
            )
            if partial_levels[later] is None:
                partial_levels[later] = update_terms
            else:
                partial_levels[later] = partial_levels[later] + update_terms
    return solution.reshape(cols_local, 1, block_size, columns_in.shape[2])


def solution(mesh):
    fine = jax.sharding.Mesh(
        mesh.devices.reshape(4, mesh.devices.shape[0] // 4, 4, mesh.devices.shape[1] // 4), PROW + PCOL
    )
    in_specs = (P(None, PROW, None, PCOL, None, None), P(None, PCOL, None, None), P(), P())
    out_specs = P(None, PCOL, None, None)
    return jax.shard_map(local, mesh=fine, in_specs=in_specs, out_specs=out_specs, check_vma=False)
```

```python
import jax
import jax.numpy as jnp
from jax import lax
from jax.sharding import PartitionSpec as P

LEVELS = 4
PROW = ("x", "core")
PCOL = ("y", "z")
RING = "z"


def node_order():
    ordering = []
    for depth_now in range(LEVELS - 1, -1, -1):
        ordering.extend(range(2**depth_now - 1, 2 ** (depth_now + 1) - 1))
    return ordering


def node_table(node_blocks, total_blocks):
    node_count = node_blocks.shape[0]
    ordered = jnp.array(node_order(), dtype=jnp.int32)
    node_ids = jnp.arange(node_count, dtype=jnp.int32)
    pick_sizes = (ordered[:, None] == node_ids[None, :]).astype(jnp.int32)
    level_sizes = jnp.sum(pick_sizes * node_blocks[None, :], axis=1)
    block_ends = jnp.cumsum(level_sizes)
    block_ids = jnp.arange(total_blocks, dtype=jnp.int32)
    positions = jnp.sum((block_ids[:, None] >= block_ends[None, :]).astype(jnp.int32), axis=1)
    return jnp.sum(
        (positions[:, None] == node_ids[None, :]).astype(jnp.int32) * ordered[None, :], axis=1
    )


def lookup(values_table, indices):
    positions_all = jnp.arange(values_table.shape[0], dtype=jnp.int32)
    return jnp.sum(
        (indices[:, None] == positions_all[None, :]).astype(jnp.int32) * values_table[None, :],
        axis=1,
    )


def panel_products(tile_stack, live_bits, vector):
    products = jnp.einsum("nxy,yw->nxw", tile_stack, vector, preferred_element_type=jnp.float32)
    return products * live_bits.astype(jnp.float32)[:, None, None]


def local(factor, right_side, node_blocks, front_mask):
    rows_local = factor.shape[0]
    cols_local = factor.shape[2]
    block_size = factor.shape[4]
    prow_count = lax.axis_size(PROW)
    pcol_count = lax.axis_size(PCOL)
    prow_index = lax.axis_index(PROW)
    pcol_index = lax.axis_index(PCOL)
    ring = lax.axis_size(RING)
    chunk_rows = block_size // ring
    total_blocks = rows_local * prow_count
    level_rows = pcol_count // prow_count
    piece_rows = block_size // pcol_count
    tile_grid = factor.reshape(rows_local, cols_local, block_size, block_size)
    tile_rows = factor.reshape(rows_local, cols_local * block_size, block_size)

    def column_tiles(first, col):
        return tile_rows[first:, col * block_size:(col + 1) * block_size]
    columns_in = right_side.reshape(cols_local, block_size, right_side.shape[3])
    block_node = node_table(node_blocks, total_blocks)
    row_ids = jnp.arange(rows_local, dtype=jnp.int32) * prow_count + prow_index
    col_ids = jnp.arange(cols_local, dtype=jnp.int32) * pcol_count + pcol_index
    row_nodes = lookup(block_node, row_ids)
    col_nodes = lookup(block_node, col_ids)
    node_ids = jnp.arange(node_blocks.shape[0], dtype=jnp.int32)
    pick_node = (col_nodes[:, None] == node_ids[None, :]).astype(jnp.int32)
    front_rows = jnp.sum(pick_node[:, :, None] * front_mask[None, :, :], axis=1)
    block_all = jnp.arange(total_blocks, dtype=jnp.int32)
    pick_row = (row_ids[:, None] == block_all[None, :]).astype(jnp.int32)
    front_bits = jnp.sum(pick_row[:, None, :] * front_rows[None, :, :], axis=2)
    diag_bits = (
        (row_nodes[:, None] == col_nodes[None, :]) & (row_ids[:, None] >= col_ids[None, :])
    ).astype(jnp.int32)

    def reduce_route(level_terms, source_bits=None):
        rhs_width = level_terms.shape[2]
        pieces = level_terms.astype(jnp.bfloat16).reshape(pcol_count, chunk_rows, rhs_width)
        got = lax.all_to_all(pieces, PCOL, 0, 0, tiled=True)
        got = got.astype(jnp.float32)
        if source_bits is not None:
            got = got * source_bits[:, None, None]
        summed = jnp.sum(got, axis=0).astype(jnp.bfloat16)
        spread = jnp.broadcast_to(summed[None], (prow_count,) + summed.shape)
        gathered = lax.all_to_all(spread, PROW, 0, 0, tiled=True)
        arrived = lax.all_to_all(gathered, RING, 0, 0, tiled=True)
        return arrived.reshape(block_size, rhs_width)

    rhs_width = columns_in.shape[2]
    partial_levels = [None] * LEVELS
    solved_list = []
    for section_now in range(LEVELS):
        first_row = section_now * level_rows
        after_row = first_row + level_rows
        if section_now == 0:
            rhs_column = columns_in[0]
        else:
            update = reduce_route(partial_levels[section_now]).astype(jnp.float32)
            rhs_column = (columns_in[section_now].astype(jnp.float32) - update).astype(jnp.bfloat16)
        if section_now == 0:
            diag_terms = jnp.einsum(
                "nxy,yw->nxw", column_tiles(0, 0)[:level_rows], rhs_column, preferred_element_type=jnp.float32
            )
            piece_row = prow_index + prow_count * (pcol_index // ring)
            sender_cols = jnp.arange(pcol_count, dtype=jnp.int32)
            piece_node = lookup(block_node, piece_row[None])
            sender_nodes = lookup(block_node, sender_cols)
            sender_bits = ((sender_nodes == piece_node) & (sender_cols <= piece_row)).astype(jnp.float32)
            solved = reduce_route(diag_terms, sender_bits)
        else:
            diag_terms = panel_products(
                column_tiles(first_row, section_now)[:level_rows],
                diag_bits[first_row:after_row, section_now],
                rhs_column,
            )
            solved = reduce_route(diag_terms)
        solved_list.append(solved)
        for later in range(section_now + 1, LEVELS):
            later_row = later * level_rows
            update_terms = panel_products(
                column_tiles(later_row, section_now)[:level_rows],
                front_bits[later_row:later_row + level_rows, section_now],
                solved,
            )
            if partial_levels[later] is None:
                partial_levels[later] = update_terms
            else:
                partial_levels[later] = partial_levels[later] + update_terms
    solution = jnp.stack(solved_list)
    return solution.reshape(cols_local, 1, block_size, columns_in.shape[2])


def solution(mesh):
    fine = jax.sharding.Mesh(
        mesh.devices.reshape(4, mesh.devices.shape[0] // 4, 4, mesh.devices.shape[1] // 4), PROW + PCOL
    )
    in_specs = (P(None, PROW, None, PCOL, None, None), P(None, PCOL, None, None), P(), P())
    out_specs = P(None, PCOL, None, None)
    return jax.shard_map(local, mesh=fine, in_specs=in_specs, out_specs=out_specs, check_vma=False)
```
